128 devices in a mesh: dp: 8 (over x, core), pair: 16 (over z, y).
Axes of the slice: x: 4, y: 4, z: 4, core: 2. Of those that a mesh axis runs over, the one named last changes fastest.
Arguments:
- anchor: bfloat16 [5, 4096, 1024], P(None, ('dp', 'pair')), may hold values from -20 to 20
- partner: bfloat16 [5, 4096, 1024], P(None, ('dp', 'pair')), may hold values from -12 to 12
- counts: int32 [5], replicated, may hold values from 512 to 4096, as said below
- pair_scale: float32 [5], replicated, may hold values from 2 to 8
Outputs:
- loss_value: float32 [], replicated
- grad_anchor: float32 [5, 4096, 1024], P(None, ('dp', 'pair'))
- grad_partner: float32 [5, 4096, 1024], P(None, ('dp', 'pair'))
The draws below stay inside these ranges and needn't reach their ends.
Inputs may be any that keep to these rules, and one draw needn't show every extreme that they name: The valid samples of pair p are its rows 0 to counts[p] - 1; one pair has all 4096 rows valid.
All inputs are finite; a program needn't handle non-finite values.
Results may differ from the reference program's by a relative error of at most 0.0021.
Values may be sent and summed in bfloat16 or wider, within the bound.
No kernel may reach another device: no remote copies, remote signals or barrier semaphores. Data moves between devices by JAX's collectives and lax.ppermute only.
A program may use at most 128 MiB of HBM per device.

```python
import math
import jax
import jax.numpy as jnp
from jax import lax

D = 1024
PAIRS = 5
PAIR_ROWS = 4096


def full_pair(key):
    return jax.random.randint(jax.random.fold_in(key, 202), (), 0, PAIRS)


def embed_pair(key):
    draw_shape = (PAIRS, PAIR_ROWS, D)
    base_draw = jnp.clip(jax.random.normal(jax.random.fold_in(key, 101), draw_shape, jnp.float32), -4.0, 4.0)
    noise_draw = jnp.clip(jax.random.normal(jax.random.fold_in(key, 102), draw_shape, jnp.float32), -4.0, 4.0)
    anchor_draw = base_draw
    partner_draw = 0.1 * base_draw + 0.99 * noise_draw
    flat_pair = full_pair(key)
    pair_ids = jnp.arange(PAIRS, dtype=jnp.int32).reshape(PAIRS, 1, 1)
    row_ids = jnp.arange(PAIR_ROWS, dtype=jnp.int32).reshape(1, PAIR_ROWS, 1)
    flat_rows = (pair_ids == flat_pair) & (row_ids >= 16)
    lift = jnp.clip(jax.random.normal(jax.random.fold_in(key, 109), (1, 1, D), jnp.float32), -4.0, 4.0)
    anchor_draw = jnp.where(flat_rows, 0.02 * anchor_draw, anchor_draw)
    partner_draw = jnp.where(flat_rows, partner_draw + lift, partner_draw)
    return (anchor_draw, partner_draw)


def draw_anchor(key, part):
    return embed_pair(key)[0].astype(jnp.bfloat16)


def draw_partner(key, part):
    return embed_pair(key)[1].astype(jnp.bfloat16)


def draw_counts(key, part):
    drawn = jax.random.randint(jax.random.fold_in(key, 201), (PAIRS,), PAIR_ROWS // 8, PAIR_ROWS + 1)
    chosen = full_pair(key)
    return jnp.where(jnp.arange(PAIRS) == chosen, PAIR_ROWS, drawn).astype(jnp.int32)


def setup_inputs(seed: int = 0) -> dict:
    splits = jax.random.split(jax.random.key(seed), 5)
    return {
        "anchor": draw_anchor(jax.random.fold_in(splits[4], 71), 0),
        "partner": draw_partner(jax.random.fold_in(splits[4], 71), 0),
        "counts": draw_counts(jax.random.fold_in(splits[4], 71), 0),
        "pair_scale": jnp.clip(jnp.exp(jax.random.uniform(splits[3], (PAIRS,), jnp.float32, math.log(2.0), math.log(8.0))), 2.0, 8.0),
    }


NEG = -1e+30

def reference(anchor, partner, counts, pair_scale):
    score_scale = 4.0 / math.sqrt(D)
    positions = jnp.arange(PAIR_ROWS, dtype=jnp.int32)
    losses = []
    anchor_grads = []
    partner_grads = []
    for pair_number in range(PAIRS):
        anchor_rows = anchor[pair_number]
        partner_rows = partner[pair_number]
        valid_count = counts[pair_number]
        row_valid = positions < valid_count
        inside = row_valid[:, None] & row_valid[None, :]
        scores = jnp.dot(anchor_rows, partner_rows.T, preferred_element_type=jnp.float32) * score_scale
        masked = jnp.where(inside, scores, NEG)
        row_high = lax.optimization_barrier(jnp.max(masked, axis=1))
        row_sum = lax.optimization_barrier(jnp.sum(jnp.where(inside, jnp.exp(masked - row_high[:, None]), 0.0), axis=1))
        row_lse = jnp.where(row_valid, row_high + jnp.log(jnp.where(row_valid, row_sum, 1.0)), 0.0)
        col_high = lax.optimization_barrier(jnp.max(masked, axis=0))
        col_sum = lax.optimization_barrier(jnp.sum(jnp.where(inside, jnp.exp(masked - col_high[None, :]), 0.0), axis=0))
        col_lse = jnp.where(row_valid, col_high + jnp.log(jnp.where(row_valid, col_sum, 1.0)), 0.0)
        positive = lax.optimization_barrier(jnp.sum(anchor_rows.astype(jnp.float32) * partner_rows.astype(jnp.float32), axis=1)) * score_scale
        loss_terms = jnp.where(row_valid, row_lse + col_lse - 2.0 * positive, 0.0)
        losses.append(jnp.sum(loss_terms) / (2.0 * valid_count.astype(jnp.float32)))
        prob_row = jnp.where(inside, jnp.exp(scores - row_lse[:, None]), 0.0)
        prob_col = jnp.where(inside, jnp.exp(scores - col_lse[None, :]), 0.0)
        weights = (pair_scale[pair_number] * 0.5 * (prob_row + prob_col)).astype(jnp.bfloat16)
        own_term = pair_scale[pair_number] * score_scale
        anchor_grad = jnp.dot(weights, partner_rows, preferred_element_type=jnp.float32) * score_scale - own_term * partner_rows.astype(jnp.float32)
        partner_grad = jnp.dot(weights.T, anchor_rows, preferred_element_type=jnp.float32) * score_scale - own_term * anchor_rows.astype(jnp.float32)
        anchor_grads.append(jnp.where(row_valid[:, None], anchor_grad, 0.0))
        partner_grads.append(jnp.where(row_valid[:, None], partner_grad, 0.0))
    loss_value = jnp.sum(jnp.stack(losses)) / PAIRS
    return (loss_value, jnp.stack(anchor_grads), jnp.stack(partner_grads))
```

```python
import math

import jax
import jax.numpy as jnp
from jax import lax
from jax.sharding import PartitionSpec as P

NEG = -1e30


def merge_gathered(stats):
    highs = stats[:, 0]
    sums = stats[:, 1]
    highest = jnp.max(highs, axis=0)
    summed = jnp.sum(sums * jnp.exp(highs - highest[None]), axis=0)
    return highest, summed


def per_device(anchor, partner, counts, pair_scale):
    pair_count, shard_rows, model_width = anchor.shape
    score_scale = 4.0 / math.sqrt(model_width)
    dp_size = lax.axis_size("dp")
    pair_size = lax.axis_size("pair")
    dp_index = lax.axis_index("dp")
    pair_place = lax.axis_index("pair")
    own_first = (dp_index * pair_size + pair_place) * shard_rows

    row_set = lax.all_gather(anchor, "pair", axis=1, tiled=True)
    col_set = lax.all_gather(partner, "dp", axis=1, tiled=True)
    row_count = row_set.shape[1]
    offsets = jnp.arange(shard_rows, dtype=jnp.int32)
    row_global = dp_index * row_count + jnp.arange(row_count, dtype=jnp.int32)
    col_first = (jnp.arange(dp_size, dtype=jnp.int32) * pair_size + pair_place) * shard_rows
    col_global = (col_first[:, None] + offsets[None, :]).reshape(-1)
    row_valid = row_global[None, :] < counts[:, None]
    col_valid = col_global[None, :] < counts[:, None]
    inside = row_valid[:, :, None] & col_valid[:, None, :]

    scores = (
        jnp.einsum("prd,pcd->prc", row_set, col_set, preferred_element_type=jnp.float32)
        * score_scale
    )
    masked = jnp.where(inside, scores, NEG)
    row_high = jnp.max(masked, axis=2)
    row_sum = jnp.sum(jnp.where(inside, jnp.exp(masked - row_high[:, :, None]), 0.0), axis=2)
    col_high = jnp.max(masked, axis=1)
    col_sum = jnp.sum(jnp.where(inside, jnp.exp(masked - col_high[:, None, :]), 0.0), axis=1)

    row_stats = lax.all_gather(jnp.stack([row_high, row_sum]), "pair")
    col_stats = lax.all_gather(jnp.stack([col_high, col_sum]), "dp")
    row_high, row_sum = merge_gathered(row_stats)
    col_high, col_sum = merge_gathered(col_stats)
    row_lse = jnp.where(row_valid, row_high + jnp.log(jnp.where(row_valid, row_sum, 1.0)), 0.0)
    col_lse = jnp.where(col_valid, col_high + jnp.log(jnp.where(col_valid, col_sum, 1.0)), 0.0)

    own_valid = own_first + offsets[None, :] < counts[:, None]
    row_own = lax.dynamic_slice_in_dim(row_lse, pair_place * shard_rows, shard_rows, 1)
    col_own = lax.dynamic_slice_in_dim(col_lse, dp_index * shard_rows, shard_rows, 1)
    positive = (
        jnp.sum(anchor.astype(jnp.float32) * partner.astype(jnp.float32), axis=2) * score_scale
    )
    loss_terms = jnp.where(own_valid, row_own + col_own - 2.0 * positive, 0.0)
    totals = lax.psum(jnp.sum(loss_terms, axis=1), ("dp", "pair"))
    loss_value = jnp.sum(totals / (2.0 * counts.astype(jnp.float32))) / pair_count

    prob_row = jnp.where(inside, jnp.exp(scores - row_lse[:, :, None]), 0.0)
    prob_col = jnp.where(inside, jnp.exp(scores - col_lse[:, None, :]), 0.0)
    weights = (pair_scale[:, None, None] * 0.5 * (prob_row + prob_col)).astype(jnp.bfloat16)
    grad_rows = (
        jnp.einsum("prc,pcd->prd", weights, col_set, preferred_element_type=jnp.float32)
        * score_scale
    )
    grad_cols = (
        jnp.einsum("prc,prd->pcd", weights, row_set, preferred_element_type=jnp.float32)
        * score_scale
    )
    anchor_part = lax.psum_scatter(grad_rows, "pair", scatter_dimension=1, tiled=True)
    partner_part = lax.psum_scatter(grad_cols, "dp", scatter_dimension=1, tiled=True)
    own_term = (pair_scale * score_scale)[:, None, None]
    keep_rows = own_valid[:, :, None]
    anchor_out = jnp.where(keep_rows, anchor_part - own_term * partner.astype(jnp.float32), 0.0)
    partner_out = jnp.where(keep_rows, partner_part - own_term * anchor.astype(jnp.float32), 0.0)
    return (loss_value, anchor_out, partner_out)


def solution(mesh):
    in_specs = (P(None, ("dp", "pair"), None), P(None, ("dp", "pair"), None), P(), P())
    out_specs = (P(), P(None, ("dp", "pair"), None), P(None, ("dp", "pair"), None))
    return jax.shard_map(
        per_device, mesh=mesh, in_specs=in_specs, out_specs=out_specs, check_vma=False
    )
```

```python
import math

import jax
import jax.numpy as jnp
from jax import lax
from jax.sharding import PartitionSpec as P

NEG = -1e30


def merge_gathered(highs, sums):
    highest = jnp.max(highs, axis=0)
    summed = jnp.sum(sums * jnp.exp(highs - highest[None]), axis=0)
    return highest, summed


def ring_position(offset, size):
    return (offset + size // 2) % size


def ring_gather(shard, axis, size):
    forward = [(i, (i + 1) % size) for i in range(size)]
    backward = [(i, (i - 1) % size) for i in range(size)]
    parts = [None] * size
    parts[ring_position(0, size)] = shard
    ahead = shard
    behind = shard
    forward_steps = size // 2
    backward_steps = size - 1 - forward_steps
    for step in range(1, forward_steps + 1):
        ahead = lax.ppermute(ahead, axis, forward)
        parts[ring_position(-step, size)] = ahead
        if step <= backward_steps:
            behind = lax.ppermute(behind, axis, backward)
            parts[ring_position(step, size)] = behind
    return parts


def ring_reduce_scatter(chunk, extra, axis, size, width):
    forward = [(i, (i + 1) % size) for i in range(size)]
    backward = [(i, (i - 1) % size) for i in range(size)]

    def ahead_part(q):
        return jnp.concatenate([chunk(q, True), extra], axis=1)

    ahead = ahead_part(ring_position(-1, size))
    behind = chunk(ring_position(1, size), False)
    for step in range(1, size):
        ahead = lax.ppermute(ahead, axis, forward) + ahead_part(ring_position(-1 - step, size))
        behind = lax.ppermute(behind, axis, backward) + chunk(ring_position(1 + step, size), False)
    rows = behind.shape[1]
    return jnp.concatenate([ahead[:, :rows], behind], axis=2), ahead[:, rows]


def per_device(anchor, partner, counts, pair_scale):
    pair_count, shard_rows, model_width = anchor.shape
    score_scale = 4.0 / math.sqrt(model_width)
    dp_size = lax.axis_size("dp")
    pair_size = lax.axis_size("pair")
    dp_index = lax.axis_index("dp")
    pair_place = lax.axis_index("pair")
    own_first = (dp_index * pair_size + pair_place) * shard_rows
    offsets = jnp.arange(shard_rows, dtype=jnp.int32)
    own_valid = own_first + offsets[None, :] < counts[:, None]
    positive = (
        jnp.sum(anchor.astype(jnp.float32) * partner.astype(jnp.float32), axis=2) * score_scale
    )
    own_positive = jnp.sum(jnp.where(own_valid, positive, 0.0), axis=1)

    row_set = lax.all_gather(anchor, "pair", axis=1, tiled=True)
    col_set = jnp.concatenate(ring_gather(partner, "dp", dp_size), axis=1)
    row_count = row_set.shape[1]
    col_count = col_set.shape[1]
    row_global = dp_index * row_count + jnp.arange(row_count, dtype=jnp.int32)
    col_owner = (dp_index + jnp.arange(dp_size, dtype=jnp.int32) - dp_size // 2) % dp_size
    col_first = (col_owner * pair_size + pair_place) * shard_rows
    col_global = (col_first[:, None] + offsets[None, :]).reshape(-1)
    row_valid = row_global[None, :] < counts[:, None]
    col_valid = col_global[None, :] < counts[:, None]
    inside = row_valid[:, :, None] & col_valid[:, None, :]

    scores = (
        jnp.einsum("prd,pcd->prc", row_set, col_set, preferred_element_type=jnp.float32)
        * score_scale
    )
    masked = jnp.where(inside, scores, NEG)
    row_high = jnp.max(masked, axis=2)
    row_sum = jnp.sum(jnp.where(inside, jnp.exp(masked - row_high[:, :, None]), 0.0), axis=2)
    col_high = jnp.max(masked, axis=1)
    col_sum = jnp.sum(jnp.where(inside, jnp.exp(masked - col_high[:, None, :]), 0.0), axis=1)

    col_stats = jnp.stack([col_high, col_sum]).reshape(2, pair_count, dp_size, shard_rows)
    col_stats = jnp.roll(col_stats, dp_index - dp_size // 2, axis=2)
    col_stats = lax.all_gather(col_stats, "dp")
    col_high, col_sum = merge_gathered(col_stats[:, 0], col_stats[:, 1])
    col_high = jnp.roll(col_high, dp_size // 2 - dp_index, axis=1).reshape(pair_count, col_count)
    col_sum = jnp.roll(col_sum, dp_size // 2 - dp_index, axis=1).reshape(pair_count, col_count)
    col_lse = jnp.where(col_valid, col_high + jnp.log(jnp.where(col_valid, col_sum, 1.0)), 0.0)

    lanes = jnp.arange(row_count, dtype=jnp.int32)[None, :]
    col_total = jnp.sum(col_lse, axis=1)
    carried = jnp.where(lanes == 0, col_total[:, None], 0.0)
    carried = jnp.where(lanes == 1, own_positive[:, None], carried)
    row_stats = lax.all_gather(jnp.stack([row_high, row_sum, carried]), "pair")
    row_high, row_sum = merge_gathered(row_stats[:, 0], row_stats[:, 1])
    carried = jnp.sum(row_stats[:, 2], axis=0)
    row_lse = jnp.where(row_valid, row_high + jnp.log(jnp.where(row_valid, row_sum, 1.0)), 0.0)
    row_part = jnp.sum(row_lse, axis=1) - 2.0 * carried[:, 1]

    prob_row = jnp.where(inside, jnp.exp(scores - row_lse[:, :, None]), 0.0)
    prob_col = jnp.where(inside, jnp.exp(scores - col_lse[:, None, :]), 0.0)
    weights = (pair_scale[:, None, None] * 0.5 * (prob_row + prob_col)).astype(jnp.bfloat16)
    grad_rows = (
        jnp.einsum("prc,pcd->prd", weights, col_set, preferred_element_type=jnp.float32)
        * score_scale
    )
    grad_cols = (
        jnp.einsum("prc,prd->pcd", weights, row_set, preferred_element_type=jnp.float32)
        * score_scale
    )
    anchor_part = lax.psum_scatter(grad_rows, "pair", scatter_dimension=1, tiled=True)

    half = model_width // 2

    def col_chunk(q, lo):
        block = grad_cols[:, q * shard_rows:(q + 1) * shard_rows]
        return block[:, :, :half] if lo else block[:, :, half:]

    width_lanes = jnp.arange(half, dtype=jnp.int32)[None, :]
    extra = jnp.where(width_lanes == dp_index, row_part[:, None], 0.0)[:, None, :]
    partner_part, row_parts = ring_reduce_scatter(col_chunk, extra, "dp", dp_size, half)

    totals = carried[:, 0] + jnp.sum(row_parts[:, :dp_size], axis=1)
    loss_value = jnp.sum(totals / (2.0 * counts.astype(jnp.float32))) / pair_count

    own_term = (pair_scale * score_scale)[:, None, None]
    keep_rows = own_valid[:, :, None]
    anchor_out = jnp.where(keep_rows, anchor_part - own_term * partner.astype(jnp.float32), 0.0)
    partner_out = jnp.where(keep_rows, partner_part - own_term * anchor.astype(jnp.float32), 0.0)
    return (loss_value, anchor_out, partner_out)


def solution(mesh):
    in_specs = (P(None, ("dp", "pair"), None), P(None, ("dp", "pair"), None), P(), P())
    out_specs = (P(), P(None, ("dp", "pair"), None), P(None, ("dp", "pair"), None))
    return jax.shard_map(
        per_device, mesh=mesh, in_specs=in_specs, out_specs=out_specs, check_vma=False
    )
```

```python
import math

import jax
import jax.numpy as jnp
from jax import lax
from jax.sharding import PartitionSpec as P

NEG = -1e30


def merge_gathered(highs, sums):
    highest = jnp.max(highs, axis=0)
    summed = jnp.sum(sums * jnp.exp(highs - highest[None]), axis=0)
    return highest, summed


def ring_position(offset, size):
    return (offset + size // 2) % size


def ring_gather(shard, axis, size):
    forward = [(i, (i + 1) % size) for i in range(size)]
    backward = [(i, (i - 1) % size) for i in range(size)]
    parts = [None] * size
    parts[ring_position(0, size)] = shard
    ahead = shard
    behind = shard
    forward_steps = size // 2
    backward_steps = size - 1 - forward_steps
    for step in range(1, forward_steps + 1):
        ahead = lax.ppermute(ahead, axis, forward)
        parts[ring_position(-step, size)] = ahead
        if step <= backward_steps:
            behind = lax.ppermute(behind, axis, backward)
            parts[ring_position(step, size)] = behind
    return parts


def two_stage_reduce_scatter(grad_cols, extra, axis, size, shard_rows):
    pair_count, _, width = grad_cols.shape
    own = lax.axis_index(axis)
    parity = own % 2
    chips = size // 2
    by_chip = grad_cols.reshape(pair_count, chips, 2, shard_rows, width)
    keep = lax.dynamic_index_in_dim(by_chip, parity, axis=2, keepdims=False)
    send = lax.dynamic_index_in_dim(by_chip, 1 - parity, axis=2, keepdims=False)
    body_rows = pair_count * chips * shard_rows
    send = jnp.concatenate([send.reshape(body_rows, width), extra], axis=0)
    got = lax.ppermute(send, axis, [(i, i ^ 1) for i in range(size)])
    summed = keep + got[:body_rows].reshape(pair_count, chips, shard_rows, width)
    carried = extra + got[body_rows:]
    chip = own // 2
    ring = [(i, (i + 2) % size) for i in range(size)]
    chunk_rows = pair_count * shard_rows

    def addend(target):
        block = lax.dynamic_index_in_dim(summed, target % chips, axis=1, keepdims=False)
        return jnp.concatenate([block.reshape(chunk_rows, width), carried], axis=0)

    running = addend(chip - 1)
    for step in range(1, chips):
        running = lax.ppermute(running, axis, ring) + addend(chip - 1 - step)
    return running[:chunk_rows].reshape(pair_count, shard_rows, width), running[chunk_rows]


def per_device(anchor, partner, counts, pair_scale):
    pair_count, shard_rows, model_width = anchor.shape
    score_scale = 4.0 / math.sqrt(model_width)
    dp_size = lax.axis_size("dp")
    pair_size = lax.axis_size("pair")
    dp_index = lax.axis_index("dp")
    pair_place = lax.axis_index("pair")
    own_first = (dp_index * pair_size + pair_place) * shard_rows
    offsets = jnp.arange(shard_rows, dtype=jnp.int32)
    own_valid = own_first + offsets[None, :] < counts[:, None]
    positive = (
        jnp.sum(anchor.astype(jnp.float32) * partner.astype(jnp.float32), axis=2) * score_scale
    )
    own_positive = jnp.sum(jnp.where(own_valid, positive, 0.0), axis=1)

    row_set = lax.all_gather(anchor, "pair", axis=1, tiled=True)
    col_set = jnp.concatenate(ring_gather(partner, "dp", dp_size), axis=1)
    col_set = jnp.roll(col_set, (dp_index - dp_size // 2) * shard_rows, axis=1)
    row_count = row_set.shape[1]
    col_count = col_set.shape[1]
    row_global = dp_index * row_count + jnp.arange(row_count, dtype=jnp.int32)
    col_first = (jnp.arange(dp_size, dtype=jnp.int32) * pair_size + pair_place) * shard_rows
    col_global = (col_first[:, None] + offsets[None, :]).reshape(-1)
    row_valid = row_global[None, :] < counts[:, None]
    col_valid = col_global[None, :] < counts[:, None]
    inside = row_valid[:, :, None] & col_valid[:, None, :]

    scores = (
        jnp.einsum("prd,pcd->prc", row_set, col_set, preferred_element_type=jnp.float32)
        * score_scale
    )
    masked = jnp.where(inside, scores, NEG)
    row_high = jnp.max(masked, axis=2)
    row_sum = jnp.sum(jnp.where(inside, jnp.exp(masked - row_high[:, :, None]), 0.0), axis=2)
    col_high = jnp.max(masked, axis=1)
    col_sum = jnp.sum(jnp.where(inside, jnp.exp(masked - col_high[:, None, :]), 0.0), axis=1)

    col_stats = lax.all_gather(jnp.stack([col_high, col_sum]), "dp")
    col_high, col_sum = merge_gathered(col_stats[:, 0], col_stats[:, 1])
    col_lse = jnp.where(col_valid, col_high + jnp.log(jnp.where(col_valid, col_sum, 1.0)), 0.0)

    lanes = jnp.arange(row_count, dtype=jnp.int32)[None, :]
    col_total = jnp.sum(col_lse, axis=1)
    carried = jnp.where(lanes == 0, col_total[:, None], 0.0)
    carried = jnp.where(lanes == 1, own_positive[:, None], carried)
    row_stats = lax.all_gather(jnp.stack([row_high, row_sum, carried]), "pair")
    row_high, row_sum = merge_gathered(row_stats[:, 0], row_stats[:, 1])
    carried = jnp.sum(row_stats[:, 2], axis=0)
    row_lse = jnp.where(row_valid, row_high + jnp.log(jnp.where(row_valid, row_sum, 1.0)), 0.0)
    row_part = jnp.sum(row_lse, axis=1) - 2.0 * carried[:, 1]

    prob_row = jnp.where(inside, jnp.exp(scores - row_lse[:, :, None]), 0.0)
    prob_col = jnp.where(inside, jnp.exp(scores - col_lse[:, None, :]), 0.0)
    weights = (pair_scale[:, None, None] * 0.5 * (prob_row + prob_col)).astype(jnp.bfloat16)
    grad_rows = (
        jnp.einsum("prc,pcd->prd", weights, col_set, preferred_element_type=jnp.float32)
        * score_scale
    )
    grad_cols = (
        jnp.einsum("prc,prd->pcd", weights, row_set, preferred_element_type=jnp.float32)
        * score_scale
    )
    anchor_part = lax.psum_scatter(grad_rows, "pair", scatter_dimension=1, tiled=True)

    width_lanes = jnp.arange(model_width, dtype=jnp.int32)[None, :]
    slots = (jnp.arange(pair_count, dtype=jnp.int32) * dp_size + dp_index)[:, None]
    loss_row = jnp.sum(jnp.where(width_lanes == slots, row_part[:, None], 0.0), axis=0)
    extra = jnp.concatenate([loss_row[None], jnp.zeros((7, model_width), jnp.float32)], axis=0)
    partner_part, loss_row = two_stage_reduce_scatter(grad_cols, extra, "dp", dp_size, shard_rows)
    row_parts = loss_row[: pair_count * dp_size].reshape(pair_count, dp_size)

    totals = carried[:, 0] + jnp.sum(row_parts, axis=1)
    loss_value = jnp.sum(totals / (2.0 * counts.astype(jnp.float32))) / pair_count

    own_term = (pair_scale * score_scale)[:, None, None]
    keep_rows = own_valid[:, :, None]
    anchor_out = jnp.where(keep_rows, anchor_part - own_term * partner.astype(jnp.float32), 0.0)
    partner_out = jnp.where(keep_rows, partner_part - own_term * anchor.astype(jnp.float32), 0.0)
    return (loss_value, anchor_out, partner_out)


def solution(mesh):
    in_specs = (P(None, ("dp", "pair"), None), P(None, ("dp", "pair"), None), P(), P())
    out_specs = (P(), P(None, ("dp", "pair"), None), P(None, ("dp", "pair"), None))
    return jax.shard_map(
        per_device, mesh=mesh, in_specs=in_specs, out_specs=out_specs, check_vma=False
    )
```

```python
import math

import jax
import jax.numpy as jnp
from jax import lax
from jax.sharding import PartitionSpec as P

NEG = -1e30


def merge_pair(mine, other):
    highest = jnp.maximum(mine[0], other[0])
    summed = mine[1] * jnp.exp(mine[0] - highest) + other[1] * jnp.exp(other[0] - highest)
    return jnp.concatenate([highest[None], summed[None], mine[2:] + other[2:]], axis=0)


def butterfly_merge(stats, axis, size):
    own = lax.axis_index(axis)
    bit = 1
    while bit < size:
        other = lax.ppermute(stats, axis, [(i, i ^ bit) for i in range(size)])
        lower = (own & bit) == 0
        stats = merge_pair(jnp.where(lower, stats, other), jnp.where(lower, other, stats))
        bit *= 2
    return stats


def ring_position(offset, size):
    return (offset + size // 2) % size


def ring_gather(shard, axis, size):
    forward = [(i, (i + 1) % size) for i in range(size)]
    backward = [(i, (i - 1) % size) for i in range(size)]
    parts = [None] * size
    parts[ring_position(0, size)] = shard
    ahead = shard
    behind = shard
    forward_steps = size // 2
    backward_steps = size - 1 - forward_steps
    for step in range(1, forward_steps + 1):
        ahead = lax.ppermute(ahead, axis, forward)
        parts[ring_position(-step, size)] = ahead
        if step <= backward_steps:
            behind = lax.ppermute(behind, axis, backward)
            parts[ring_position(step, size)] = behind
    return parts


def two_stage_reduce_scatter(grad_cols, extra, axis, size, shard_rows):
    pair_count, _, width = grad_cols.shape
    own = lax.axis_index(axis)
    parity = own % 2
    chips = size // 2
    by_chip = grad_cols.reshape(pair_count, chips, 2, shard_rows, width)
    keep = lax.dynamic_index_in_dim(by_chip, parity, axis=2, keepdims=False)
    send = lax.dynamic_index_in_dim(by_chip, 1 - parity, axis=2, keepdims=False)
    body_rows = pair_count * chips * shard_rows
    send = jnp.concatenate([send.reshape(body_rows, width), extra], axis=0)
    got = lax.ppermute(send, axis, [(i, i ^ 1) for i in range(size)])
    summed = keep + got[:body_rows].reshape(pair_count, chips, shard_rows, width)
    carried = extra + got[body_rows:]
    chip = own // 2
    ring = [(i, (i + 2) % size) for i in range(size)]
    chunk_rows = pair_count * shard_rows

    def addend(target):
        block = lax.dynamic_index_in_dim(summed, target % chips, axis=1, keepdims=False)
        return jnp.concatenate([block.reshape(chunk_rows, width), carried], axis=0)

    running = addend(chip - 1)
    for step in range(1, chips):
        running = lax.ppermute(running, axis, ring) + addend(chip - 1 - step)
    return running[:chunk_rows].reshape(pair_count, shard_rows, width), running[chunk_rows]


def per_device(anchor, partner, counts, pair_scale):
    pair_count, shard_rows, model_width = anchor.shape
    score_scale = 4.0 / math.sqrt(model_width)
    dp_size = lax.axis_size("dp")
    pair_size = lax.axis_size("pair")
    dp_index = lax.axis_index("dp")
    pair_place = lax.axis_index("pair")
    own_first = (dp_index * pair_size + pair_place) * shard_rows
    offsets = jnp.arange(shard_rows, dtype=jnp.int32)
    own_valid = own_first + offsets[None, :] < counts[:, None]
    positive = (
        jnp.sum(anchor.astype(jnp.float32) * partner.astype(jnp.float32), axis=2) * score_scale
    )
    own_positive = jnp.sum(jnp.where(own_valid, positive, 0.0), axis=1)

    row_set = lax.all_gather(anchor, "pair", axis=1, tiled=True)
    col_set = jnp.concatenate(ring_gather(partner, "dp", dp_size), axis=1)
    col_set = jnp.roll(col_set, (dp_index - dp_size // 2) * shard_rows, axis=1)
    row_count = row_set.shape[1]
    col_count = col_set.shape[1]
    row_global = dp_index * row_count + jnp.arange(row_count, dtype=jnp.int32)
    col_first = (jnp.arange(dp_size, dtype=jnp.int32) * pair_size + pair_place) * shard_rows
    col_global = (col_first[:, None] + offsets[None, :]).reshape(-1)
    row_valid = row_global[None, :] < counts[:, None]
    col_valid = col_global[None, :] < counts[:, None]
    inside = row_valid[:, :, None] & col_valid[:, None, :]

    scores = (
        jnp.einsum("prd,pcd->prc", row_set, col_set, preferred_element_type=jnp.float32)
        * score_scale
    )
    masked = jnp.where(inside, scores, NEG)
    row_high = jnp.max(masked, axis=2)
    row_sum = jnp.sum(jnp.where(inside, jnp.exp(masked - row_high[:, :, None]), 0.0), axis=2)
    col_high = jnp.max(masked, axis=1)
    col_sum = jnp.sum(jnp.where(inside, jnp.exp(masked - col_high[:, None, :]), 0.0), axis=1)

    col_stats = butterfly_merge(jnp.stack([col_high, col_sum]), "dp", dp_size)
    col_high, col_sum = col_stats[0], col_stats[1]
    col_lse = jnp.where(col_valid, col_high + jnp.log(jnp.where(col_valid, col_sum, 1.0)), 0.0)

    lanes = jnp.arange(row_count, dtype=jnp.int32)[None, :]
    col_total = jnp.sum(col_lse, axis=1)
    carried = jnp.where(lanes == 0, col_total[:, None], 0.0)
    carried = jnp.where(lanes == 1, own_positive[:, None], carried)
    row_stats = butterfly_merge(jnp.stack([row_high, row_sum, carried]), "pair", pair_size)
    row_high, row_sum, carried = row_stats[0], row_stats[1], row_stats[2]
    row_lse = jnp.where(row_valid, row_high + jnp.log(jnp.where(row_valid, row_sum, 1.0)), 0.0)
    row_part = jnp.sum(row_lse, axis=1) - 2.0 * carried[:, 1]

    prob_row = jnp.where(inside, jnp.exp(scores - row_lse[:, :, None]), 0.0)
    prob_col = jnp.where(inside, jnp.exp(scores - col_lse[:, None, :]), 0.0)
    weights = (pair_scale[:, None, None] * 0.5 * (prob_row + prob_col)).astype(jnp.bfloat16)
    grad_rows = (
        jnp.einsum("prc,pcd->prd", weights, col_set, preferred_element_type=jnp.float32)
        * score_scale
    )
    grad_cols = (
        jnp.einsum("prc,prd->pcd", weights, row_set, preferred_element_type=jnp.float32)
        * score_scale
    )
    anchor_part = lax.psum_scatter(grad_rows, "pair", scatter_dimension=1, tiled=True)

    width_lanes = jnp.arange(model_width, dtype=jnp.int32)[None, :]
    slots = (jnp.arange(pair_count, dtype=jnp.int32) * dp_size + dp_index)[:, None]
    loss_row = jnp.sum(jnp.where(width_lanes == slots, row_part[:, None], 0.0), axis=0)
    extra = jnp.concatenate([loss_row[None], jnp.zeros((7, model_width), jnp.float32)], axis=0)
    partner_part, loss_row = two_stage_reduce_scatter(grad_cols, extra, "dp", dp_size, shard_rows)
    row_parts = loss_row[: pair_count * dp_size].reshape(pair_count, dp_size)

    totals = carried[:, 0] + jnp.sum(row_parts, axis=1)
    loss_value = jnp.sum(totals / (2.0 * counts.astype(jnp.float32))) / pair_count

    own_term = (pair_scale * score_scale)[:, None, None]
    keep_rows = own_valid[:, :, None]
    anchor_out = jnp.where(keep_rows, anchor_part - own_term * partner.astype(jnp.float32), 0.0)
    partner_out = jnp.where(keep_rows, partner_part - own_term * anchor.astype(jnp.float32), 0.0)
    return (loss_value, anchor_out, partner_out)


def solution(mesh):
    in_specs = (P(None, ("dp", "pair"), None), P(None, ("dp", "pair"), None), P(), P())
    out_specs = (P(), P(None, ("dp", "pair"), None), P(None, ("dp", "pair"), None))
    return jax.shard_map(
        per_device, mesh=mesh, in_specs=in_specs, out_specs=out_specs, check_vma=False
    )
```

```python
import math

import jax
import jax.numpy as jnp
from jax import lax
from jax.sharding import PartitionSpec as P

NEG = -1e30


def merge_pair(mine, other):
    highest = jnp.maximum(mine[0], other[0])
    summed = mine[1] * jnp.exp(mine[0] - highest) + other[1] * jnp.exp(other[0] - highest)
    return jnp.concatenate([highest[None], summed[None], mine[2:] + other[2:]], axis=0)


def butterfly_merge(stats, axis, size):
    own = lax.axis_index(axis)
    bit = 1
    while bit < size:
        other = lax.ppermute(stats, axis, [(i, i ^ bit) for i in range(size)])
        lower = (own & bit) == 0
        stats = merge_pair(jnp.where(lower, stats, other), jnp.where(lower, other, stats))
        bit *= 2
    return stats


def butterfly_sum(values, axis, size):
    own = lax.axis_index(axis)
    bit = 1
    while bit < size:
        other = lax.ppermute(values, axis, [(i, i ^ bit) for i in range(size)])
        lower = (own & bit) == 0
        values = jnp.where(lower, values, other) + jnp.where(lower, other, values)
        bit *= 2
    return values


def ring_position(offset, size):
    return (offset + size // 2) % size


def ring_gather(shard, axis, size):
    forward = [(i, (i + 1) % size) for i in range(size)]
    backward = [(i, (i - 1) % size) for i in range(size)]
    parts = [None] * size
    parts[ring_position(0, size)] = shard
    ahead = shard
    behind = shard
    forward_steps = size // 2
    backward_steps = size - 1 - forward_steps
    for step in range(1, forward_steps + 1):
        ahead = lax.ppermute(ahead, axis, forward)
        parts[ring_position(-step, size)] = ahead
        if step <= backward_steps:
            behind = lax.ppermute(behind, axis, backward)
            parts[ring_position(step, size)] = behind
    return parts


def two_stage_reduce_scatter(grad_cols, extra, axis, size, shard_rows):
    pair_count, _, width = grad_cols.shape
    own = lax.axis_index(axis)
    parity = own % 2
    chips = size // 2
    by_chip = grad_cols.reshape(pair_count, chips, 2, shard_rows, width)
    keep = lax.dynamic_index_in_dim(by_chip, parity, axis=2, keepdims=False)
    send = lax.dynamic_index_in_dim(by_chip, 1 - parity, axis=2, keepdims=False)
    body_rows = pair_count * chips * shard_rows
    send = jnp.concatenate([send.reshape(body_rows, width), extra], axis=0)
    got = lax.ppermute(send, axis, [(i, i ^ 1) for i in range(size)])
    summed = keep + got[:body_rows].reshape(pair_count, chips, shard_rows, width)
    carried = extra + got[body_rows:]
    chip = own // 2
    ring = [(i, (i + 2) % size) for i in range(size)]
    chunk_rows = pair_count * shard_rows

    def addend(target):
        block = lax.dynamic_index_in_dim(summed, target % chips, axis=1, keepdims=False)
        return jnp.concatenate([block.reshape(chunk_rows, width), carried], axis=0)

    running = addend(chip - 1)
    for step in range(1, chips):
        running = lax.ppermute(running, axis, ring) + addend(chip - 1 - step)
    return running[:chunk_rows].reshape(pair_count, shard_rows, width), running[chunk_rows]


def per_device(anchor, partner, counts, pair_scale):
    pair_count, shard_rows, model_width = anchor.shape
    score_scale = 4.0 / math.sqrt(model_width)
    dp_size = lax.axis_size("dp")
    pair_size = lax.axis_size("pair")
    dp_index = lax.axis_index("dp")
    pair_place = lax.axis_index("pair")
    own_first = (dp_index * pair_size + pair_place) * shard_rows
    offsets = jnp.arange(shard_rows, dtype=jnp.int32)
    own_valid = own_first + offsets[None, :] < counts[:, None]
    positive = (
        jnp.sum(anchor.astype(jnp.float32) * partner.astype(jnp.float32), axis=2) * score_scale
    )
    own_positive = jnp.sum(jnp.where(own_valid, positive, 0.0), axis=1)

    row_set = lax.all_gather(anchor, "pair", axis=1, tiled=True)
    col_set = jnp.concatenate(ring_gather(partner, "dp", dp_size), axis=1)
    col_set = jnp.roll(col_set, (dp_index - dp_size // 2) * shard_rows, axis=1)
    row_count = row_set.shape[1]
    col_count = col_set.shape[1]
    row_global = dp_index * row_count + jnp.arange(row_count, dtype=jnp.int32)
    col_first = (jnp.arange(dp_size, dtype=jnp.int32) * pair_size + pair_place) * shard_rows
    col_global = (col_first[:, None] + offsets[None, :]).reshape(-1)
    row_valid = row_global[None, :] < counts[:, None]
    col_valid = col_global[None, :] < counts[:, None]
    inside = row_valid[:, :, None] & col_valid[:, None, :]

    scores = (
        jnp.einsum("prd,pcd->prc", row_set, col_set, preferred_element_type=jnp.float32)
        * score_scale
    )
    masked = jnp.where(inside, scores, NEG)
    row_high = jnp.max(masked, axis=2)
    row_sum = jnp.sum(jnp.where(inside, jnp.exp(masked - row_high[:, :, None]), 0.0), axis=2)
    col_high = jnp.max(masked, axis=1)
    col_sum = jnp.sum(jnp.where(inside, jnp.exp(masked - col_high[:, None, :]), 0.0), axis=1)

    col_stats = butterfly_merge(jnp.stack([col_high, col_sum]), "dp", dp_size)
    col_high, col_sum = col_stats[0], col_stats[1]
    col_lse = jnp.where(col_valid, col_high + jnp.log(jnp.where(col_valid, col_sum, 1.0)), 0.0)

    lanes = jnp.arange(row_count, dtype=jnp.int32)[None, :]
    carried = jnp.where(lanes == 0, own_positive[:, None], 0.0)
    row_stats = butterfly_merge(jnp.stack([row_high, row_sum, carried]), "pair", pair_size)
    row_high, row_sum, carried = row_stats[0], row_stats[1], row_stats[2]
    row_lse = jnp.where(row_valid, row_high + jnp.log(jnp.where(row_valid, row_sum, 1.0)), 0.0)
    row_part = jnp.sum(row_lse, axis=1) - 2.0 * carried[:, 0]

    prob_row = jnp.where(inside, jnp.exp(scores - row_lse[:, :, None]), 0.0)
    prob_col = jnp.where(inside, jnp.exp(scores - col_lse[:, None, :]), 0.0)
    weights = (pair_scale[:, None, None] * 0.5 * (prob_row + prob_col)).astype(jnp.bfloat16)
    grad_rows = (
        jnp.einsum("prc,pcd->prd", weights, col_set, preferred_element_type=jnp.float32)
        * score_scale
    )
    grad_cols = (
        jnp.einsum("prc,prd->pcd", weights, row_set, preferred_element_type=jnp.float32)
        * score_scale
    )
    anchor_part = lax.psum_scatter(grad_rows, "pair", scatter_dimension=1, tiled=True)

    width_lanes = jnp.arange(model_width, dtype=jnp.int32)[None, :]
    slots = (jnp.arange(pair_count, dtype=jnp.int32) * dp_size + dp_index)[:, None]
    loss_row = jnp.sum(jnp.where(width_lanes == slots, row_part[:, None], 0.0), axis=0)
    extra = jnp.concatenate([loss_row[None], jnp.zeros((7, model_width), jnp.float32)], axis=0)
    partner_part, loss_row = two_stage_reduce_scatter(grad_cols, extra, "dp", dp_size, shard_rows)
    row_parts = loss_row[: pair_count * dp_size].reshape(pair_count, dp_size)

    col_total = butterfly_sum(jnp.sum(col_lse, axis=1), "pair", pair_size)
    totals = col_total + jnp.sum(row_parts, axis=1)
    loss_value = jnp.sum(totals / (2.0 * counts.astype(jnp.float32))) / pair_count

    own_term = (pair_scale * score_scale)[:, None, None]
    keep_rows = own_valid[:, :, None]
    anchor_out = jnp.where(keep_rows, anchor_part - own_term * partner.astype(jnp.float32), 0.0)
    partner_out = jnp.where(keep_rows, partner_part - own_term * anchor.astype(jnp.float32), 0.0)
    return (loss_value, anchor_out, partner_out)


def solution(mesh):
    in_specs = (P(None, ("dp", "pair"), None), P(None, ("dp", "pair"), None), P(), P())
    out_specs = (P(), P(None, ("dp", "pair"), None), P(None, ("dp", "pair"), None))
    return jax.shard_map(
        per_device, mesh=mesh, in_specs=in_specs, out_specs=out_specs, check_vma=False
    )
```

```python
import math

import jax
import jax.numpy as jnp
from jax import lax
from jax.sharding import PartitionSpec as P

NEG = -1e30


def merge_pair(mine, other):
    highest = jnp.maximum(mine[0], other[0])
    summed = mine[1] * jnp.exp(mine[0] - highest) + other[1] * jnp.exp(other[0] - highest)
    return jnp.concatenate([highest[None], summed[None], mine[2:] + other[2:]], axis=0)


def butterfly_merge(stats, axis, size):
    own = lax.axis_index(axis)
    bit = 1
    while bit < size:
        other = lax.ppermute(stats, axis, [(i, i ^ bit) for i in range(size)])
        lower = (own & bit) == 0
        stats = merge_pair(jnp.where(lower, stats, other), jnp.where(lower, other, stats))
        bit *= 2
    return stats


def butterfly_sum(values, axis, size):
    own = lax.axis_index(axis)
    bit = 1
    while bit < size:
        other = lax.ppermute(values, axis, [(i, i ^ bit) for i in range(size)])
        lower = (own & bit) == 0
        values = jnp.where(lower, values, other) + jnp.where(lower, other, values)
        bit *= 2
    return values


def ring_position(offset, size):
    return (offset + size // 2) % size


def ring_gather(shard, axis, size):
    forward = [(i, (i + 1) % size) for i in range(size)]
    backward = [(i, (i - 1) % size) for i in range(size)]
    parts = [None] * size
    parts[ring_position(0, size)] = shard
    ahead = shard
    behind = shard
    forward_steps = size // 2
    backward_steps = size - 1 - forward_steps
    for step in range(1, forward_steps + 1):
        ahead = lax.ppermute(ahead, axis, forward)
        parts[ring_position(-step, size)] = ahead
        if step <= backward_steps:
            behind = lax.ppermute(behind, axis, backward)
            parts[ring_position(step, size)] = behind
    return parts


def two_stage_reduce_scatter(grad_cols, extra, axis, size, shard_rows):
    pair_count, _, width = grad_cols.shape
    own = lax.axis_index(axis)
    parity = own % 2
    chips = size // 2
    by_chip = grad_cols.reshape(pair_count, chips, 2, shard_rows, width)
    keep = lax.dynamic_index_in_dim(by_chip, parity, axis=2, keepdims=False)
    send = lax.dynamic_index_in_dim(by_chip, 1 - parity, axis=2, keepdims=False)
    body_rows = pair_count * chips * shard_rows
    send = jnp.concatenate([send.reshape(body_rows, width), extra], axis=0)
    got = lax.ppermute(send, axis, [(i, i ^ 1) for i in range(size)])
    summed = keep + got[:body_rows].reshape(pair_count, chips, shard_rows, width)
    carried = extra + got[body_rows:]
    chip = own // 2
    ring = [(i, (i + 2) % size) for i in range(size)]
    chunk_rows = pair_count * shard_rows

    def addend(target):
        block = lax.dynamic_index_in_dim(summed, target % chips, axis=1, keepdims=False)
        return jnp.concatenate([block.reshape(chunk_rows, width), carried], axis=0)

    running = addend(chip - 1)
    for step in range(1, chips):
        running = lax.ppermute(running, axis, ring) + addend(chip - 1 - step)
    return running[:chunk_rows].reshape(pair_count, shard_rows, width), running[chunk_rows]


def per_device(anchor, partner, counts, pair_scale):
    pair_count, shard_rows, model_width = anchor.shape
    score_scale = 4.0 / math.sqrt(model_width)
    dp_size = lax.axis_size("dp")
    pair_size = lax.axis_size("pair")
    dp_index = lax.axis_index("dp")
    pair_place = lax.axis_index("pair")
    own_first = (dp_index * pair_size + pair_place) * shard_rows
    offsets = jnp.arange(shard_rows, dtype=jnp.int32)
    own_valid = own_first + offsets[None, :] < counts[:, None]
    positive = (
        jnp.sum(anchor.astype(jnp.float32) * partner.astype(jnp.float32), axis=2) * score_scale
    )
    own_positive = jnp.sum(jnp.where(own_valid, positive, 0.0), axis=1)

    row_set = lax.all_gather(anchor, "pair", axis=1, tiled=True)
    col_set = jnp.concatenate(ring_gather(partner, "dp", dp_size), axis=1)
    col_set = jnp.roll(col_set, (dp_index - dp_size // 2) * shard_rows, axis=1)
    row_count = row_set.shape[1]
    col_count = col_set.shape[1]
    row_global = dp_index * row_count + jnp.arange(row_count, dtype=jnp.int32)
    col_first = (jnp.arange(dp_size, dtype=jnp.int32) * pair_size + pair_place) * shard_rows
    col_global = (col_first[:, None] + offsets[None, :]).reshape(-1)
    row_valid = row_global[None, :] < counts[:, None]
    col_valid = col_global[None, :] < counts[:, None]
    inside = row_valid[:, :, None] & col_valid[:, None, :]

    scores = (
        jnp.einsum("prd,pcd->prc", row_set, col_set, preferred_element_type=jnp.float32)
        * score_scale
    )
    masked = jnp.where(inside, scores, NEG)
    row_high = jnp.max(masked, axis=2)
    row_sum = jnp.sum(jnp.where(inside, jnp.exp(masked - row_high[:, :, None]), 0.0), axis=2)
    col_high = jnp.max(masked, axis=1)
    col_sum = jnp.sum(jnp.where(inside, jnp.exp(masked - col_high[:, None, :]), 0.0), axis=1)

    col_stats = butterfly_merge(jnp.stack([col_high, col_sum]), "dp", dp_size)
    col_high, col_sum = col_stats[0], col_stats[1]
    col_lse = jnp.where(col_valid, col_high + jnp.log(jnp.where(col_valid, col_sum, 1.0)), 0.0)

    lanes = jnp.arange(row_count, dtype=jnp.int32)[None, :]
    carried = jnp.where(lanes == 0, own_positive[:, None], 0.0)
    row_stats = butterfly_merge(jnp.stack([row_high, row_sum, carried]), "pair", pair_size)
    row_high, row_sum, carried = row_stats[0], row_stats[1], row_stats[2]
    row_lse = jnp.where(row_valid, row_high + jnp.log(jnp.where(row_valid, row_sum, 1.0)), 0.0)
    row_part = jnp.sum(row_lse, axis=1) - 2.0 * carried[:, 0]

    prob_row = jnp.where(inside, jnp.exp(scores - row_lse[:, :, None]), 0.0)
    prob_col = jnp.where(inside, jnp.exp(scores - col_lse[:, None, :]), 0.0)
    weights = (pair_scale[:, None, None] * 0.5 * (prob_row + prob_col)).astype(jnp.bfloat16)
    weights = lax.optimization_barrier(weights)
    grad_rows = (
        jnp.einsum("prc,pcd->prd", weights, col_set, preferred_element_type=jnp.float32)
        * score_scale
    )
    grad_cols = (
        jnp.einsum("prc,prd->pcd", weights, row_set, preferred_element_type=jnp.float32)
        * score_scale
    )
    anchor_part = lax.psum_scatter(grad_rows, "pair", scatter_dimension=1, tiled=True)

    width_lanes = jnp.arange(model_width, dtype=jnp.int32)[None, :]
    slots = (jnp.arange(pair_count, dtype=jnp.int32) * dp_size + dp_index)[:, None]
    loss_row = jnp.sum(jnp.where(width_lanes == slots, row_part[:, None], 0.0), axis=0)
    extra = jnp.concatenate([loss_row[None], jnp.zeros((7, model_width), jnp.float32)], axis=0)
    partner_part, loss_row = two_stage_reduce_scatter(grad_cols, extra, "dp", dp_size, shard_rows)
    row_parts = loss_row[: pair_count * dp_size].reshape(pair_count, dp_size)

    col_total = butterfly_sum(jnp.sum(col_lse, axis=1), "pair", pair_size)
    totals = col_total + jnp.sum(row_parts, axis=1)
    loss_value = jnp.sum(totals / (2.0 * counts.astype(jnp.float32))) / pair_count

    own_term = (pair_scale * score_scale)[:, None, None]
    keep_rows = own_valid[:, :, None]
    anchor_out = jnp.where(keep_rows, anchor_part - own_term * partner.astype(jnp.float32), 0.0)
    partner_out = jnp.where(keep_rows, partner_part - own_term * anchor.astype(jnp.float32), 0.0)
    return (loss_value, anchor_out, partner_out)


def solution(mesh):
    in_specs = (P(None, ("dp", "pair"), None), P(None, ("dp", "pair"), None), P(), P())
    out_specs = (P(), P(None, ("dp", "pair"), None), P(None, ("dp", "pair"), None))
    return jax.shard_map(
        per_device, mesh=mesh, in_specs=in_specs, out_specs=out_specs, check_vma=False
    )
```

```python
import math

import jax
import jax.numpy as jnp
from jax import lax
from jax.sharding import PartitionSpec as P

NEG = -1e30


def merge_pair(mine, other):
    highest = jnp.maximum(mine[0], other[0])
    summed = mine[1] * jnp.exp(mine[0] - highest) + other[1] * jnp.exp(other[0] - highest)
    return jnp.concatenate([highest[None], summed[None], mine[2:] + other[2:]], axis=0)


def butterfly_merge(stats, axis, size):
    own = lax.axis_index(axis)
    bit = 1
    while bit < size:
        other = lax.ppermute(stats, axis, [(i, i ^ bit) for i in range(size)])
        lower = (own & bit) == 0
        stats = merge_pair(jnp.where(lower, stats, other), jnp.where(lower, other, stats))
        bit *= 2
    return stats


def group_merge(stats, axis, stride, group):
    own = lax.axis_index(axis)
    digit = (own // stride) % group
    size = lax.axis_size(axis)
    received = [stats]
    for shift in range(1, group):
        perm = [(i, i + ((i // stride + shift) % group - (i // stride) % group) * stride)
                for i in range(size)]
        received.append(lax.ppermute(stats, axis, perm))
    stacked = jnp.stack(received)
    ordered = jnp.take(stacked, (digit - jnp.arange(group)) % group, axis=0)
    merged = ordered[0]
    for member in range(1, group):
        merged = merge_pair(merged, ordered[member])
    return merged


def butterfly_sum(values, axis, size):
    own = lax.axis_index(axis)
    bit = 1
    while bit < size:
        other = lax.ppermute(values, axis, [(i, i ^ bit) for i in range(size)])
        lower = (own & bit) == 0
        values = jnp.where(lower, values, other) + jnp.where(lower, other, values)
        bit *= 2
    return values


def ring_position(offset, size):
    return (offset + size // 2) % size


def ring_gather(shard, axis, size):
    forward = [(i, (i + 1) % size) for i in range(size)]
    backward = [(i, (i - 1) % size) for i in range(size)]
    parts = [None] * size
    parts[ring_position(0, size)] = shard
    ahead = shard
    behind = shard
    forward_steps = size // 2
    backward_steps = size - 1 - forward_steps
    for step in range(1, forward_steps + 1):
        ahead = lax.ppermute(ahead, axis, forward)
        parts[ring_position(-step, size)] = ahead
        if step <= backward_steps:
            behind = lax.ppermute(behind, axis, backward)
            parts[ring_position(step, size)] = behind
    return parts


def two_stage_reduce_scatter(grad_cols, extra, axis, size, shard_rows):
    pair_count, _, width = grad_cols.shape
    own = lax.axis_index(axis)
    parity = own % 2
    chips = size // 2
    by_chip = grad_cols.reshape(pair_count, chips, 2, shard_rows, width)
    keep = lax.dynamic_index_in_dim(by_chip, parity, axis=2, keepdims=False)
    send = lax.dynamic_index_in_dim(by_chip, 1 - parity, axis=2, keepdims=False)
    body_rows = pair_count * chips * shard_rows
    send = jnp.concatenate([send.reshape(body_rows, width), extra], axis=0)
    got = lax.ppermute(send, axis, [(i, i ^ 1) for i in range(size)])
    summed = keep + got[:body_rows].reshape(pair_count, chips, shard_rows, width)
    carried = extra + got[body_rows:]
    chip = own // 2
    ring = [(i, (i + 2) % size) for i in range(size)]
    chunk_rows = pair_count * shard_rows

    def addend(target):
        block = lax.dynamic_index_in_dim(summed, target % chips, axis=1, keepdims=False)
        return jnp.concatenate([block.reshape(chunk_rows, width), carried], axis=0)

    running = addend(chip - 1)
    for step in range(1, chips):
        running = lax.ppermute(running, axis, ring) + addend(chip - 1 - step)
    return running[:chunk_rows].reshape(pair_count, shard_rows, width), running[chunk_rows]


def per_device(anchor, partner, counts, pair_scale):
    pair_count, shard_rows, model_width = anchor.shape
    score_scale = 4.0 / math.sqrt(model_width)
    dp_size = lax.axis_size("dp")
    pair_size = lax.axis_size("pair")
    dp_index = lax.axis_index("dp")
    pair_place = lax.axis_index("pair")
    own_first = (dp_index * pair_size + pair_place) * shard_rows
    offsets = jnp.arange(shard_rows, dtype=jnp.int32)
    own_valid = own_first + offsets[None, :] < counts[:, None]
    positive = (
        jnp.sum(anchor.astype(jnp.float32) * partner.astype(jnp.float32), axis=2) * score_scale
    )
    own_positive = jnp.sum(jnp.where(own_valid, positive, 0.0), axis=1)

    row_set = lax.all_gather(anchor, "pair", axis=1, tiled=True)
    col_set = jnp.concatenate(ring_gather(partner, "dp", dp_size), axis=1)
    col_set = jnp.roll(col_set, (dp_index - dp_size // 2) * shard_rows, axis=1)
    row_count = row_set.shape[1]
    col_count = col_set.shape[1]
    row_global = dp_index * row_count + jnp.arange(row_count, dtype=jnp.int32)
    col_first = (jnp.arange(dp_size, dtype=jnp.int32) * pair_size + pair_place) * shard_rows
    col_global = (col_first[:, None] + offsets[None, :]).reshape(-1)
    row_valid = row_global[None, :] < counts[:, None]
    col_valid = col_global[None, :] < counts[:, None]
    inside = row_valid[:, :, None] & col_valid[:, None, :]

    scores = (
        jnp.einsum("prd,pcd->prc", row_set, col_set, preferred_element_type=jnp.float32)
        * score_scale
    )
    masked = jnp.where(inside, scores, NEG)
    row_high = jnp.max(masked, axis=2)
    row_sum = jnp.sum(jnp.where(inside, jnp.exp(masked - row_high[:, :, None]), 0.0), axis=2)
    col_high = jnp.max(masked, axis=1)
    col_sum = jnp.sum(jnp.where(inside, jnp.exp(masked - col_high[:, None, :]), 0.0), axis=1)

    col_stats = jnp.stack([col_high, col_sum])
    col_stats = group_merge(group_merge(col_stats, "dp", 1, 2), "dp", 2, dp_size // 2)
    col_high, col_sum = col_stats[0], col_stats[1]
    col_lse = jnp.where(col_valid, col_high + jnp.log(jnp.where(col_valid, col_sum, 1.0)), 0.0)

    lanes = jnp.arange(row_count, dtype=jnp.int32)[None, :]
    carried = jnp.where(lanes == 0, own_positive[:, None], 0.0)
    row_stats = jnp.stack([row_high, row_sum, carried])
    row_stats = group_merge(group_merge(row_stats, "pair", 1, 4), "pair", 4, pair_size // 4)
    row_high, row_sum, carried = row_stats[0], row_stats[1], row_stats[2]
    row_lse = jnp.where(row_valid, row_high + jnp.log(jnp.where(row_valid, row_sum, 1.0)), 0.0)
    row_part = jnp.sum(row_lse, axis=1) - 2.0 * carried[:, 0]

    prob_row = jnp.where(inside, jnp.exp(scores - row_lse[:, :, None]), 0.0)
    prob_col = jnp.where(inside, jnp.exp(scores - col_lse[:, None, :]), 0.0)
    weights = (pair_scale[:, None, None] * 0.5 * (prob_row + prob_col)).astype(jnp.bfloat16)
    weights = lax.optimization_barrier(weights)
    grad_rows = (
        jnp.einsum("prc,pcd->prd", weights, col_set, preferred_element_type=jnp.float32)
        * score_scale
    )
    grad_cols = (
        jnp.einsum("prc,prd->pcd", weights, row_set, preferred_element_type=jnp.float32)
        * score_scale
    )
    anchor_part = lax.psum_scatter(grad_rows, "pair", scatter_dimension=1, tiled=True)

    width_lanes = jnp.arange(model_width, dtype=jnp.int32)[None, :]
    slots = (jnp.arange(pair_count, dtype=jnp.int32) * dp_size + dp_index)[:, None]
    loss_row = jnp.sum(jnp.where(width_lanes == slots, row_part[:, None], 0.0), axis=0)
    extra = jnp.concatenate([loss_row[None], jnp.zeros((7, model_width), jnp.float32)], axis=0)
    partner_part, loss_row = two_stage_reduce_scatter(grad_cols, extra, "dp", dp_size, shard_rows)
    row_parts = loss_row[: pair_count * dp_size].reshape(pair_count, dp_size)

    col_total = butterfly_sum(jnp.sum(col_lse, axis=1), "pair", pair_size)
    totals = col_total + jnp.sum(row_parts, axis=1)
    loss_value = jnp.sum(totals / (2.0 * counts.astype(jnp.float32))) / pair_count

    own_term = (pair_scale * score_scale)[:, None, None]
    keep_rows = own_valid[:, :, None]
    anchor_out = jnp.where(keep_rows, anchor_part - own_term * partner.astype(jnp.float32), 0.0)
    partner_out = jnp.where(keep_rows, partner_part - own_term * anchor.astype(jnp.float32), 0.0)
    return (loss_value, anchor_out, partner_out)


def solution(mesh):
    in_specs = (P(None, ("dp", "pair"), None), P(None, ("dp", "pair"), None), P(), P())
    out_specs = (P(), P(None, ("dp", "pair"), None), P(None, ("dp", "pair"), None))
    return jax.shard_map(
        per_device, mesh=mesh, in_specs=in_specs, out_specs=out_specs, check_vma=False
    )
```

```python
import math

import jax
import jax.numpy as jnp
from jax import lax
from jax.sharding import Mesh, PartitionSpec as P

NEG = -1e30
PAIR = ("pz", "py")


def merge_pair(mine, other):
    highest = jnp.maximum(mine[0], other[0])
    summed = mine[1] * jnp.exp(mine[0] - highest) + other[1] * jnp.exp(other[0] - highest)
    return jnp.concatenate([highest[None], summed[None], mine[2:] + other[2:]], axis=0)


def butterfly_merge(stats, axis, size):
    own = lax.axis_index(axis)
    bit = 1
    while bit < size:
        other = lax.ppermute(stats, axis, [(i, i ^ bit) for i in range(size)])
        lower = (own & bit) == 0
        stats = merge_pair(jnp.where(lower, stats, other), jnp.where(lower, other, stats))
        bit *= 2
    return stats


def group_merge(stats, axis, stride, group):
    own = lax.axis_index(axis)
    digit = (own // stride) % group
    size = lax.axis_size(axis)
    received = [stats]
    for shift in range(1, group):
        perm = [(i, i + ((i // stride + shift) % group - (i // stride) % group) * stride)
                for i in range(size)]
        received.append(lax.ppermute(stats, axis, perm))
    stacked = jnp.stack(received)
    ordered = jnp.take(stacked, (digit - jnp.arange(group)) % group, axis=0)
    merged = ordered[0]
    for member in range(1, group):
        merged = merge_pair(merged, ordered[member])
    return merged


def butterfly_sum(values, axis, size):
    own = lax.axis_index(axis)
    bit = 1
    while bit < size:
        other = lax.ppermute(values, axis, [(i, i ^ bit) for i in range(size)])
        lower = (own & bit) == 0
        values = jnp.where(lower, values, other) + jnp.where(lower, other, values)
        bit *= 2
    return values


def ring_position(offset, size):
    return (offset + size // 2) % size


def ring_gather(shard, axis, size):
    forward = [(i, (i + 1) % size) for i in range(size)]
    backward = [(i, (i - 1) % size) for i in range(size)]
    parts = [None] * size
    parts[ring_position(0, size)] = shard
    ahead = shard
    behind = shard
    forward_steps = size // 2
    backward_steps = size - 1 - forward_steps
    for step in range(1, forward_steps + 1):
        ahead = lax.ppermute(ahead, axis, forward)
        parts[ring_position(-step, size)] = ahead
        if step <= backward_steps:
            behind = lax.ppermute(behind, axis, backward)
            parts[ring_position(step, size)] = behind
    return parts


def two_stage_reduce_scatter(grad_cols, extra, axis, size, shard_rows):
    pair_count, _, width = grad_cols.shape
    own = lax.axis_index(axis)
    parity = own % 2
    chips = size // 2
    by_chip = grad_cols.reshape(pair_count, chips, 2, shard_rows, width)
    keep = lax.dynamic_index_in_dim(by_chip, parity, axis=2, keepdims=False)
    send = lax.dynamic_index_in_dim(by_chip, 1 - parity, axis=2, keepdims=False)
    body_rows = pair_count * chips * shard_rows
    send = jnp.concatenate([send.reshape(body_rows, width), extra], axis=0)
    got = lax.ppermute(send, axis, [(i, i ^ 1) for i in range(size)])
    summed = keep + got[:body_rows].reshape(pair_count, chips, shard_rows, width)
    carried = extra + got[body_rows:]
    chip = own // 2
    ring = [(i, (i + 2) % size) for i in range(size)]
    chunk_rows = pair_count * shard_rows

    def addend(target):
        block = lax.dynamic_index_in_dim(summed, target % chips, axis=1, keepdims=False)
        return jnp.concatenate([block.reshape(chunk_rows, width), carried], axis=0)

    running = addend(chip - 1)
    for step in range(1, chips):
        running = lax.ppermute(running, axis, ring) + addend(chip - 1 - step)
    return running[:chunk_rows].reshape(pair_count, shard_rows, width), running[chunk_rows]


def per_device(anchor, partner, counts, pair_scale):
    pair_count, shard_rows, model_width = anchor.shape
    score_scale = 4.0 / math.sqrt(model_width)
    dp_size = lax.axis_size("dp")
    pair_size = lax.axis_size(PAIR)
    dp_index = lax.axis_index("dp")
    pair_place = lax.axis_index(PAIR)
    own_first = (dp_index * pair_size + pair_place) * shard_rows
    offsets = jnp.arange(shard_rows, dtype=jnp.int32)
    own_valid = own_first + offsets[None, :] < counts[:, None]
    positive = (
        jnp.sum(anchor.astype(jnp.float32) * partner.astype(jnp.float32), axis=2) * score_scale
    )
    own_positive = jnp.sum(jnp.where(own_valid, positive, 0.0), axis=1)

    row_set = lax.all_gather(anchor, "py", axis=1, tiled=True)
    row_set = lax.all_gather(row_set, "pz", axis=1, tiled=True)
    col_set = jnp.concatenate(ring_gather(partner, "dp", dp_size), axis=1)
    col_set = jnp.roll(col_set, (dp_index - dp_size // 2) * shard_rows, axis=1)
    row_count = row_set.shape[1]
    col_count = col_set.shape[1]
    row_global = dp_index * row_count + jnp.arange(row_count, dtype=jnp.int32)
    col_first = (jnp.arange(dp_size, dtype=jnp.int32) * pair_size + pair_place) * shard_rows
    col_global = (col_first[:, None] + offsets[None, :]).reshape(-1)
    row_valid = row_global[None, :] < counts[:, None]
    col_valid = col_global[None, :] < counts[:, None]
    inside = row_valid[:, :, None] & col_valid[:, None, :]

    scores = (
        jnp.einsum("prd,pcd->prc", row_set, col_set, preferred_element_type=jnp.float32)
        * score_scale
    )
    masked = jnp.where(inside, scores, NEG)
    row_high = jnp.max(masked, axis=2)
    row_sum = jnp.sum(jnp.where(inside, jnp.exp(masked - row_high[:, :, None]), 0.0), axis=2)
    col_high = jnp.max(masked, axis=1)
    col_sum = jnp.sum(jnp.where(inside, jnp.exp(masked - col_high[:, None, :]), 0.0), axis=1)

    col_stats = jnp.stack([col_high, col_sum])
    col_stats = group_merge(group_merge(col_stats, "dp", 1, 2), "dp", 2, dp_size // 2)
    col_high, col_sum = col_stats[0], col_stats[1]
    col_lse = jnp.where(col_valid, col_high + jnp.log(jnp.where(col_valid, col_sum, 1.0)), 0.0)

    lanes = jnp.arange(row_count, dtype=jnp.int32)[None, :]
    carried = jnp.where(lanes == 0, own_positive[:, None], 0.0)
    row_stats = jnp.stack([row_high, row_sum, carried])
    row_stats = group_merge(group_merge(row_stats, PAIR, 1, 4), PAIR, 4, pair_size // 4)
    row_high, row_sum, carried = row_stats[0], row_stats[1], row_stats[2]
    row_lse = jnp.where(row_valid, row_high + jnp.log(jnp.where(row_valid, row_sum, 1.0)), 0.0)
    row_part = jnp.sum(row_lse, axis=1) - 2.0 * carried[:, 0]

    prob_row = jnp.where(inside, jnp.exp(scores - row_lse[:, :, None]), 0.0)
    prob_col = jnp.where(inside, jnp.exp(scores - col_lse[:, None, :]), 0.0)
    weights = (pair_scale[:, None, None] * 0.5 * (prob_row + prob_col)).astype(jnp.bfloat16)
    weights = lax.optimization_barrier(weights)
    grad_rows = (
        jnp.einsum("prc,pcd->prd", weights, col_set, preferred_element_type=jnp.float32)
        * score_scale
    )
    grad_cols = (
        jnp.einsum("prc,prd->pcd", weights, row_set, preferred_element_type=jnp.float32)
        * score_scale
    )
    anchor_part = lax.psum_scatter(grad_rows, "pz", scatter_dimension=1, tiled=True)
    anchor_part = lax.psum_scatter(anchor_part, "py", scatter_dimension=1, tiled=True)

    width_lanes = jnp.arange(model_width, dtype=jnp.int32)[None, :]
    slots = (jnp.arange(pair_count, dtype=jnp.int32) * dp_size + dp_index)[:, None]
    loss_row = jnp.sum(jnp.where(width_lanes == slots, row_part[:, None], 0.0), axis=0)
    extra = jnp.concatenate([loss_row[None], jnp.zeros((7, model_width), jnp.float32)], axis=0)
    partner_part, loss_row = two_stage_reduce_scatter(grad_cols, extra, "dp", dp_size, shard_rows)
    row_parts = loss_row[: pair_count * dp_size].reshape(pair_count, dp_size)

    col_total = butterfly_sum(jnp.sum(col_lse, axis=1), PAIR, pair_size)
    totals = col_total + jnp.sum(row_parts, axis=1)
    loss_value = jnp.sum(totals / (2.0 * counts.astype(jnp.float32))) / pair_count

    own_term = (pair_scale * score_scale)[:, None, None]
    keep_rows = own_valid[:, :, None]
    anchor_out = jnp.where(keep_rows, anchor_part - own_term * partner.astype(jnp.float32), 0.0)
    partner_out = jnp.where(keep_rows, partner_part - own_term * anchor.astype(jnp.float32), 0.0)
    return (loss_value, anchor_out, partner_out)


def solution(mesh):
    dp_size, pair_size = mesh.devices.shape
    side = math.isqrt(pair_size)
    split = Mesh(mesh.devices.reshape(dp_size, pair_size // side, side), ("dp",) + PAIR)
    rows = P(None, ("dp",) + PAIR, None)
    in_specs = (rows, rows, P(), P())
    out_specs = (P(), rows, rows)
    return jax.shard_map(
        per_device, mesh=split, in_specs=in_specs, out_specs=out_specs, check_vma=False
    )
```

```python
import math

import jax
import jax.numpy as jnp
from jax import lax
from jax.sharding import PartitionSpec as P

NEG = -1e30


def merge_pair(mine, other):
    highest = jnp.maximum(mine[0], other[0])
    summed = mine[1] * jnp.exp(mine[0] - highest) + other[1] * jnp.exp(other[0] - highest)
    return jnp.concatenate([highest[None], summed[None], mine[2:] + other[2:]], axis=0)


def butterfly_merge(stats, axis, size):
    own = lax.axis_index(axis)
    bit = 1
    while bit < size:
        other = lax.ppermute(stats, axis, [(i, i ^ bit) for i in range(size)])
        lower = (own & bit) == 0
        stats = merge_pair(jnp.where(lower, stats, other), jnp.where(lower, other, stats))
        bit *= 2
    return stats


def butterfly_sum(values, axis, size):
    own = lax.axis_index(axis)
    bit = 1
    while bit < size:
        other = lax.ppermute(values, axis, [(i, i ^ bit) for i in range(size)])
        lower = (own & bit) == 0
        values = jnp.where(lower, values, other) + jnp.where(lower, other, values)
        bit *= 2
    return values


def ring_position(offset, size):
    return (offset + size // 2) % size


def ring_gather(shard, axis, size):
    forward = [(i, (i + 1) % size) for i in range(size)]
    backward = [(i, (i - 1) % size) for i in range(size)]
    parts = [None] * size
    parts[ring_position(0, size)] = shard
    ahead = shard
    behind = shard
    forward_steps = size // 2
    backward_steps = size - 1 - forward_steps
    for step in range(1, forward_steps + 1):
        ahead = lax.ppermute(ahead, axis, forward)
        parts[ring_position(-step, size)] = ahead
        if step <= backward_steps:
            behind = lax.ppermute(behind, axis, backward)
            parts[ring_position(step, size)] = behind
    return parts


def two_stage_reduce_scatter(grad_cols, extra, axis, size, shard_rows):
    pair_count, _, width = grad_cols.shape
    own = lax.axis_index(axis)
    parity = own % 2
    chips = size // 2
    by_chip = grad_cols.reshape(pair_count, chips, 2, shard_rows, width)
    keep = lax.dynamic_index_in_dim(by_chip, parity, axis=2, keepdims=False)
    send = lax.dynamic_index_in_dim(by_chip, 1 - parity, axis=2, keepdims=False)
    body_rows = pair_count * chips * shard_rows
    send = jnp.concatenate([send.reshape(body_rows, width), extra], axis=0)
    got = lax.ppermute(send, axis, [(i, i ^ 1) for i in range(size)])
    summed = keep + got[:body_rows].reshape(pair_count, chips, shard_rows, width)
    carried = extra + got[body_rows:]
    chip = own // 2
    ring = [(i, (i + 2) % size) for i in range(size)]
    chunk_rows = pair_count * shard_rows

    def addend(target):
        block = lax.dynamic_index_in_dim(summed, target % chips, axis=1, keepdims=False)
        return jnp.concatenate([block.reshape(chunk_rows, width), carried], axis=0)

    running = addend(chip - 1)
    for step in range(1, chips):
        running = lax.ppermute(running, axis, ring) + addend(chip - 1 - step)
    return running[:chunk_rows].reshape(pair_count, shard_rows, width), running[chunk_rows]


def per_device(anchor, partner, counts, pair_scale):
    pair_count, shard_rows, model_width = anchor.shape
    score_scale = 4.0 / math.sqrt(model_width)
    dp_size = lax.axis_size("dp")
    pair_size = lax.axis_size("pair")
    dp_index = lax.axis_index("dp")
    pair_place = lax.axis_index("pair")
    own_first = (dp_index * pair_size + pair_place) * shard_rows
    offsets = jnp.arange(shard_rows, dtype=jnp.int32)
    own_valid = own_first + offsets[None, :] < counts[:, None]
    positive = (
        jnp.sum(anchor.astype(jnp.float32) * partner.astype(jnp.float32), axis=2) * score_scale
    )
    own_positive = jnp.sum(jnp.where(own_valid, positive, 0.0), axis=1)

    row_set = lax.all_gather(anchor, "pair", axis=1, tiled=True)
    col_set = jnp.concatenate(ring_gather(partner, "dp", dp_size), axis=1)
    col_set = jnp.roll(col_set, (dp_index - dp_size // 2) * shard_rows, axis=1)
    row_count = row_set.shape[1]
    col_count = col_set.shape[1]
    row_global = dp_index * row_count + jnp.arange(row_count, dtype=jnp.int32)
    col_first = (jnp.arange(dp_size, dtype=jnp.int32) * pair_size + pair_place) * shard_rows
    col_global = (col_first[:, None] + offsets[None, :]).reshape(-1)
    row_valid = row_global[None, :] < counts[:, None]
    col_valid = col_global[None, :] < counts[:, None]
    inside = row_valid[:, :, None] & col_valid[:, None, :]

    scores = (
        jnp.einsum("prd,pcd->prc", row_set, col_set, preferred_element_type=jnp.float32)
        * score_scale
    )
    masked = jnp.where(inside, scores, NEG)
    row_high = jnp.max(masked, axis=2)
    row_sum = jnp.sum(jnp.where(inside, jnp.exp(masked - row_high[:, :, None]), 0.0), axis=2)
    col_high = jnp.max(masked, axis=1)
    col_sum = jnp.sum(jnp.where(inside, jnp.exp(masked - col_high[:, None, :]), 0.0), axis=1)

    col_stats = butterfly_merge(jnp.stack([col_high, col_sum]), "dp", dp_size)
    col_high, col_sum = col_stats[0], col_stats[1]
    col_lse = jnp.where(col_valid, col_high + jnp.log(jnp.where(col_valid, col_sum, 1.0)), 0.0)

    lanes = jnp.arange(row_count, dtype=jnp.int32)[None, :]
    carried = jnp.where(lanes == 0, own_positive[:, None], 0.0)
    row_stats = butterfly_merge(jnp.stack([row_high, row_sum, carried]), "pair", pair_size)
    row_high, row_sum, carried = row_stats[0], row_stats[1], row_stats[2]
    row_lse = jnp.where(row_valid, row_high + jnp.log(jnp.where(row_valid, row_sum, 1.0)), 0.0)
    row_part = jnp.sum(row_lse, axis=1) - 2.0 * carried[:, 0]

    prob_row = jnp.where(inside, jnp.exp(scores - row_lse[:, :, None]), 0.0)
    prob_col = jnp.where(inside, jnp.exp(scores - col_lse[:, None, :]), 0.0)
    weights = (pair_scale[:, None, None] * 0.5 * (prob_row + prob_col)).astype(jnp.bfloat16)
    weights = lax.optimization_barrier(weights)
    grad_rows = (
        jnp.einsum("prc,pcd->prd", weights, col_set, preferred_element_type=jnp.float32)
        * score_scale
    )
    grad_cols = (
        jnp.einsum("prc,prd->pcd", weights, row_set, preferred_element_type=jnp.float32)
        * score_scale
    )
    own_term = (pair_scale * score_scale)[:, None, None]
    own_start = pair_place * shard_rows
    own_chunk = lax.dynamic_slice_in_dim(grad_rows, own_start, shard_rows, 1)
    own_chunk = own_chunk - own_term * partner.astype(jnp.float32)
    grad_rows = lax.dynamic_update_slice_in_dim(grad_rows, own_chunk, own_start, 1)
    grad_rows = jnp.where(row_valid[:, :, None], grad_rows, 0.0)
    anchor_out = lax.psum_scatter(grad_rows, "pair", scatter_dimension=1, tiled=True)

    width_lanes = jnp.arange(model_width, dtype=jnp.int32)[None, :]
    slots = (jnp.arange(pair_count, dtype=jnp.int32) * dp_size + dp_index)[:, None]
    loss_row = jnp.sum(jnp.where(width_lanes == slots, row_part[:, None], 0.0), axis=0)
    extra = jnp.concatenate([loss_row[None], jnp.zeros((7, model_width), jnp.float32)], axis=0)
    partner_part, loss_row = two_stage_reduce_scatter(grad_cols, extra, "dp", dp_size, shard_rows)
    row_parts = loss_row[: pair_count * dp_size].reshape(pair_count, dp_size)

    col_total = butterfly_sum(jnp.sum(col_lse, axis=1), "pair", pair_size)
    totals = col_total + jnp.sum(row_parts, axis=1)
    loss_value = jnp.sum(totals / (2.0 * counts.astype(jnp.float32))) / pair_count

    keep_rows = own_valid[:, :, None]
    partner_out = jnp.where(keep_rows, partner_part - own_term * anchor.astype(jnp.float32), 0.0)
    return (loss_value, anchor_out, partner_out)


def solution(mesh):
    in_specs = (P(None, ("dp", "pair"), None), P(None, ("dp", "pair"), None), P(), P())
    out_specs = (P(), P(None, ("dp", "pair"), None), P(None, ("dp", "pair"), None))
    return jax.shard_map(
        per_device, mesh=mesh, in_specs=in_specs, out_specs=out_specs, check_vma=False
    )
```

```python
import math

import jax
import jax.numpy as jnp
from jax import lax
from jax.sharding import PartitionSpec as P

NEG = -1e30


def merge_pair(mine, other):
    highest = jnp.maximum(mine[0], other[0])
    summed = mine[1] * jnp.exp(mine[0] - highest) + other[1] * jnp.exp(other[0] - highest)
    return jnp.concatenate([highest[None], summed[None], mine[2:] + other[2:]], axis=0)


def butterfly_merge(stats, axis, size):
    own = lax.axis_index(axis)
    bit = 1
    while bit < size:
        other = lax.ppermute(stats, axis, [(i, i ^ bit) for i in range(size)])
        lower = (own & bit) == 0
        stats = merge_pair(jnp.where(lower, stats, other), jnp.where(lower, other, stats))
        bit *= 2
    return stats


def butterfly_sum(values, axis, size):
    own = lax.axis_index(axis)
    bit = 1
    while bit < size:
        other = lax.ppermute(values, axis, [(i, i ^ bit) for i in range(size)])
        lower = (own & bit) == 0
        values = jnp.where(lower, values, other) + jnp.where(lower, other, values)
        bit *= 2
    return values


def ring_position(offset, size):
    return (offset + size // 2) % size


def ring_gather(shard, axis, size):
    forward = [(i, (i + 1) % size) for i in range(size)]
    backward = [(i, (i - 1) % size) for i in range(size)]
    parts = [None] * size
    parts[ring_position(0, size)] = shard
    ahead = shard
    behind = shard
    forward_steps = size // 2
    backward_steps = size - 1 - forward_steps
    for step in range(1, forward_steps + 1):
        ahead = lax.ppermute(ahead, axis, forward)
        parts[ring_position(-step, size)] = ahead
        if step <= backward_steps:
            behind = lax.ppermute(behind, axis, backward)
            parts[ring_position(step, size)] = behind
    return parts


def two_stage_reduce_scatter(grad_cols, extra, axis, size, shard_rows):
    pair_count, _, width = grad_cols.shape
    own = lax.axis_index(axis)
    parity = own % 2
    chips = size // 2
    by_chip = grad_cols.reshape(pair_count, chips, 2, shard_rows, width)
    keep = lax.dynamic_index_in_dim(by_chip, parity, axis=2, keepdims=False)
    send = lax.dynamic_index_in_dim(by_chip, 1 - parity, axis=2, keepdims=False)
    body_rows = pair_count * chips * shard_rows
    send = jnp.concatenate([send.reshape(body_rows, width), extra], axis=0)
    got = lax.ppermute(send, axis, [(i, i ^ 1) for i in range(size)])
    summed = keep + got[:body_rows].reshape(pair_count, chips, shard_rows, width)
    carried = extra + got[body_rows:]
    chip = own // 2
    ring = [(i, (i + 2) % size) for i in range(size)]
    chunk_rows = pair_count * shard_rows

    def addend(target):
        block = lax.dynamic_index_in_dim(summed, target % chips, axis=1, keepdims=False)
        return jnp.concatenate([block.reshape(chunk_rows, width), carried], axis=0)

    running = addend(chip - 1)
    for step in range(1, chips):
        running = lax.ppermute(running, axis, ring) + addend(chip - 1 - step)
    return running[:chunk_rows].reshape(pair_count, shard_rows, width), running[chunk_rows]


def per_device(anchor, partner, counts, pair_scale):
    pair_count, shard_rows, model_width = anchor.shape
    score_scale = 4.0 / math.sqrt(model_width)
    dp_size = lax.axis_size("dp")
    pair_size = lax.axis_size("pair")
    dp_index = lax.axis_index("dp")
    pair_place = lax.axis_index("pair")
    own_first = (dp_index * pair_size + pair_place) * shard_rows
    offsets = jnp.arange(shard_rows, dtype=jnp.int32)
    own_valid = own_first + offsets[None, :] < counts[:, None]
    positive = (
        jnp.sum(anchor.astype(jnp.float32) * partner.astype(jnp.float32), axis=2) * score_scale
    )
    own_positive = jnp.sum(jnp.where(own_valid, positive, 0.0), axis=1)

    row_set = lax.all_gather(anchor, "pair", axis=1, tiled=True)
    col_set = jnp.concatenate(ring_gather(partner, "dp", dp_size), axis=1)
    col_set = jnp.roll(col_set, (dp_index - dp_size // 2) * shard_rows, axis=1)
    row_count = row_set.shape[1]
    col_count = col_set.shape[1]
    row_global = dp_index * row_count + jnp.arange(row_count, dtype=jnp.int32)
    col_first = (jnp.arange(dp_size, dtype=jnp.int32) * pair_size + pair_place) * shard_rows
    col_global = (col_first[:, None] + offsets[None, :]).reshape(-1)
    row_valid = row_global[None, :] < counts[:, None]
    col_valid = col_global[None, :] < counts[:, None]
    inside = row_valid[:, :, None] & col_valid[:, None, :]

    scores = (
        jnp.einsum("prd,pcd->prc", row_set, col_set, preferred_element_type=jnp.float32)
        * score_scale
    )
    masked = jnp.where(inside, scores, NEG)
    row_high = jnp.max(masked, axis=2)
    row_sum = jnp.sum(jnp.where(inside, jnp.exp(masked - row_high[:, :, None]), 0.0), axis=2)
    col_high = jnp.max(masked, axis=1)
    col_sum = jnp.sum(jnp.where(inside, jnp.exp(masked - col_high[:, None, :]), 0.0), axis=1)

    col_stats = butterfly_merge(jnp.stack([col_high, col_sum]), "dp", dp_size)
    col_high, col_sum = col_stats[0], col_stats[1]
    col_lse = jnp.where(col_valid, col_high + jnp.log(jnp.where(col_valid, col_sum, 1.0)), 0.0)

    lanes = jnp.arange(row_count, dtype=jnp.int32)[None, :]
    carried = jnp.where(lanes == 0, own_positive[:, None], 0.0)
    row_stats = butterfly_merge(jnp.stack([row_high, row_sum, carried]), "pair", pair_size)
    row_high, row_sum, carried = row_stats[0], row_stats[1], row_stats[2]
    row_lse = jnp.where(row_valid, row_high + jnp.log(jnp.where(row_valid, row_sum, 1.0)), 0.0)
    row_part = jnp.sum(row_lse, axis=1) - 2.0 * carried[:, 0]

    prob_row = jnp.where(inside, jnp.exp(scores - row_lse[:, :, None]), 0.0)
    prob_col = jnp.where(inside, jnp.exp(scores - col_lse[:, None, :]), 0.0)
    weights = (pair_scale[:, None, None] * 0.5 * (prob_row + prob_col)).astype(jnp.bfloat16)
    weights = lax.optimization_barrier(weights)
    grad_rows = (
        jnp.einsum("prc,pcd->prd", weights, col_set, preferred_element_type=jnp.float32)
        * score_scale
    )
    grad_cols = (
        jnp.einsum("prc,prd->pcd", weights, row_set, preferred_element_type=jnp.float32)
        * score_scale
    )
    anchor_part = lax.psum_scatter(grad_rows, "pair", scatter_dimension=1, tiled=True)

    width_lanes = jnp.arange(model_width, dtype=jnp.int32)[None, :]
    slots = (jnp.arange(pair_count, dtype=jnp.int32) * dp_size + dp_index)[:, None]
    loss_row = jnp.sum(jnp.where(width_lanes == slots, row_part[:, None], 0.0), axis=0)
    extra = jnp.concatenate([loss_row[None], jnp.zeros((7, model_width), jnp.float32)], axis=0)
    partner_part, loss_row = two_stage_reduce_scatter(grad_cols, extra, "dp", dp_size, shard_rows)
    row_parts = loss_row[: pair_count * dp_size].reshape(pair_count, dp_size)

    col_total = butterfly_sum(jnp.sum(col_lse, axis=1), "pair", pair_size)
    totals = col_total + jnp.sum(row_parts, axis=1)
    loss_value = jnp.sum(totals / (2.0 * counts.astype(jnp.float32))) / pair_count

    own_term = (pair_scale * score_scale)[:, None, None]
    keep_rows = own_valid[:, :, None]
    partner_out = jnp.where(keep_rows, partner_part - own_term * anchor.astype(jnp.float32), 0.0)
    anchor_part, partner_out = lax.optimization_barrier((anchor_part, partner_out))
    anchor_out = jnp.where(keep_rows, anchor_part - own_term * partner.astype(jnp.float32), 0.0)
    return (loss_value, anchor_out, partner_out)


def solution(mesh):
    in_specs = (P(None, ("dp", "pair"), None), P(None, ("dp", "pair"), None), P(), P())
    out_specs = (P(), P(None, ("dp", "pair"), None), P(None, ("dp", "pair"), None))
    return jax.shard_map(
        per_device, mesh=mesh, in_specs=in_specs, out_specs=out_specs, check_vma=False
    )
```

```python
import math

import jax
import jax.numpy as jnp
from jax import lax
from jax.sharding import PartitionSpec as P

NEG = -1e30


def merge_pair(mine, other):
    highest = jnp.maximum(mine[0], other[0])
    summed = mine[1] * jnp.exp(mine[0] - highest) + other[1] * jnp.exp(other[0] - highest)
    return jnp.concatenate([highest[None], summed[None], mine[2:] + other[2:]], axis=0)


def butterfly_merge(stats, axis, size):
    own = lax.axis_index(axis)
    bit = 1
    while bit < size:
        other = lax.ppermute(stats, axis, [(i, i ^ bit) for i in range(size)])
        lower = (own & bit) == 0
        stats = merge_pair(jnp.where(lower, stats, other), jnp.where(lower, other, stats))
        bit *= 2
    return stats


def butterfly_sum(values, axis, size):
    own = lax.axis_index(axis)
    bit = 1
    while bit < size:
        other = lax.ppermute(values, axis, [(i, i ^ bit) for i in range(size)])
        lower = (own & bit) == 0
        values = jnp.where(lower, values, other) + jnp.where(lower, other, values)
        bit *= 2
    return values


def ring_position(offset, size):
    return (offset + size // 2) % size


def ring_gather(shard, axis, size):
    forward = [(i, (i + 1) % size) for i in range(size)]
    backward = [(i, (i - 1) % size) for i in range(size)]
    parts = [None] * size
    parts[ring_position(0, size)] = shard
    ahead = shard
    behind = shard
    forward_steps = size // 2
    backward_steps = size - 1 - forward_steps
    for step in range(1, forward_steps + 1):
        ahead = lax.ppermute(ahead, axis, forward)
        parts[ring_position(-step, size)] = ahead
        if step <= backward_steps:
            behind = lax.ppermute(behind, axis, backward)
            parts[ring_position(step, size)] = behind
    return parts


def two_stage_reduce_scatter(grad_cols, extra, axis, size, shard_rows):
    pair_count, _, width = grad_cols.shape
    own = lax.axis_index(axis)
    parity = own % 2
    chips = size // 2
    by_chip = grad_cols.reshape(pair_count, chips, 2, shard_rows, width)
    keep = lax.dynamic_index_in_dim(by_chip, parity, axis=2, keepdims=False)
    send = lax.dynamic_index_in_dim(by_chip, 1 - parity, axis=2, keepdims=False)
    body_rows = pair_count * chips * shard_rows
    send = jnp.concatenate([send.reshape(body_rows, width), extra], axis=0)
    got = lax.ppermute(send, axis, [(i, i ^ 1) for i in range(size)])
    summed = keep + got[:body_rows].reshape(pair_count, chips, shard_rows, width)
    carried = extra + got[body_rows:]
    chip = own // 2
    ring = [(i, (i + 2) % size) for i in range(size)]
    chunk_rows = pair_count * shard_rows

    def addend(target):
        block = lax.dynamic_index_in_dim(summed, target % chips, axis=1, keepdims=False)
        return jnp.concatenate([block.reshape(chunk_rows, width), carried], axis=0)

    running = addend(chip - 1)
    for step in range(1, chips):
        running = lax.ppermute(running, axis, ring) + addend(chip - 1 - step)
    return running[:chunk_rows].reshape(pair_count, shard_rows, width), running[chunk_rows]


def per_device(anchor, partner, counts, pair_scale):
    pair_count, shard_rows, model_width = anchor.shape
    score_scale = 4.0 / math.sqrt(model_width)
    dp_size = lax.axis_size("dp")
    pair_size = lax.axis_size("pair")
    dp_index = lax.axis_index("dp")
    pair_place = lax.axis_index("pair")
    own_first = (dp_index * pair_size + pair_place) * shard_rows
    offsets = jnp.arange(shard_rows, dtype=jnp.int32)
    own_valid = own_first + offsets[None, :] < counts[:, None]
    positive = (
        jnp.sum(anchor.astype(jnp.float32) * partner.astype(jnp.float32), axis=2) * score_scale
    )
    own_positive = jnp.sum(jnp.where(own_valid, positive, 0.0), axis=1)

    row_blocks = lax.all_gather(anchor, "pair", axis=0)
    col_set = jnp.concatenate(ring_gather(partner, "dp", dp_size), axis=1)
    col_set = jnp.roll(col_set, (dp_index - dp_size // 2) * shard_rows, axis=1)
    row_count = row_blocks.shape[0] * shard_rows
    col_count = col_set.shape[1]
    row_global = dp_index * row_count + jnp.arange(row_count, dtype=jnp.int32)
    col_first = (jnp.arange(dp_size, dtype=jnp.int32) * pair_size + pair_place) * shard_rows
    col_global = (col_first[:, None] + offsets[None, :]).reshape(-1)
    row_valid = row_global[None, :] < counts[:, None]
    col_valid = col_global[None, :] < counts[:, None]
    inside = row_valid[:, :, None] & col_valid[:, None, :]

    scores = (
        jnp.einsum("kprd,pcd->pkrc", row_blocks, col_set, preferred_element_type=jnp.float32)
        * score_scale
    ).reshape(pair_count, row_count, col_count)
    masked = jnp.where(inside, scores, NEG)
    row_high = jnp.max(masked, axis=2)
    row_sum = jnp.sum(jnp.where(inside, jnp.exp(masked - row_high[:, :, None]), 0.0), axis=2)
    col_high = jnp.max(masked, axis=1)
    col_sum = jnp.sum(jnp.where(inside, jnp.exp(masked - col_high[:, None, :]), 0.0), axis=1)

    col_stats = butterfly_merge(jnp.stack([col_high, col_sum]), "dp", dp_size)
    col_high, col_sum = col_stats[0], col_stats[1]
    col_lse = jnp.where(col_valid, col_high + jnp.log(jnp.where(col_valid, col_sum, 1.0)), 0.0)

    lanes = jnp.arange(row_count, dtype=jnp.int32)[None, :]
    carried = jnp.where(lanes == 0, own_positive[:, None], 0.0)
    row_stats = butterfly_merge(jnp.stack([row_high, row_sum, carried]), "pair", pair_size)
    row_high, row_sum, carried = row_stats[0], row_stats[1], row_stats[2]
    row_lse = jnp.where(row_valid, row_high + jnp.log(jnp.where(row_valid, row_sum, 1.0)), 0.0)
    row_part = jnp.sum(row_lse, axis=1) - 2.0 * carried[:, 0]

    prob_row = jnp.where(inside, jnp.exp(scores - row_lse[:, :, None]), 0.0)
    prob_col = jnp.where(inside, jnp.exp(scores - col_lse[:, None, :]), 0.0)
    weights = (pair_scale[:, None, None] * 0.5 * (prob_row + prob_col)).astype(jnp.bfloat16)
    weights = lax.optimization_barrier(weights)
    weight_blocks = weights.reshape(pair_count, pair_size, shard_rows, col_count)
    grad_rows = (
        jnp.einsum("pkrc,pcd->kprd", weight_blocks, col_set, preferred_element_type=jnp.float32)
        * score_scale
    )
    grad_cols = (
        jnp.einsum("pkrc,kprd->pcd", weight_blocks, row_blocks, preferred_element_type=jnp.float32)
        * score_scale
    )
    anchor_part = lax.psum_scatter(
        grad_rows.reshape(-1, model_width), "pair", scatter_dimension=0, tiled=True
    ).reshape(pair_count, shard_rows, model_width)

    width_lanes = jnp.arange(model_width, dtype=jnp.int32)[None, :]
    slots = (jnp.arange(pair_count, dtype=jnp.int32) * dp_size + dp_index)[:, None]
    loss_row = jnp.sum(jnp.where(width_lanes == slots, row_part[:, None], 0.0), axis=0)
    extra = jnp.concatenate([loss_row[None], jnp.zeros((7, model_width), jnp.float32)], axis=0)
    partner_part, loss_row = two_stage_reduce_scatter(grad_cols, extra, "dp", dp_size, shard_rows)
    row_parts = loss_row[: pair_count * dp_size].reshape(pair_count, dp_size)

    col_total = butterfly_sum(jnp.sum(col_lse, axis=1), "pair", pair_size)
    totals = col_total + jnp.sum(row_parts, axis=1)
    loss_value = jnp.sum(totals / (2.0 * counts.astype(jnp.float32))) / pair_count

    own_term = (pair_scale * score_scale)[:, None, None]
    keep_rows = own_valid[:, :, None]
    anchor_out = jnp.where(keep_rows, anchor_part - own_term * partner.astype(jnp.float32), 0.0)
    partner_out = jnp.where(keep_rows, partner_part - own_term * anchor.astype(jnp.float32), 0.0)
    return (loss_value, anchor_out, partner_out)


def solution(mesh):
    in_specs = (P(None, ("dp", "pair"), None), P(None, ("dp", "pair"), None), P(), P())
    out_specs = (P(), P(None, ("dp", "pair"), None), P(None, ("dp", "pair"), None))
    return jax.shard_map(
        per_device, mesh=mesh, in_specs=in_specs, out_specs=out_specs, check_vma=False
    )
```

```python
import math

import jax
import jax.numpy as jnp
from jax import lax
from jax.sharding import PartitionSpec as P

NEG = -1e30


def merge_pair(mine, other):
    highest = jnp.maximum(mine[0], other[0])
    summed = mine[1] * jnp.exp(mine[0] - highest) + other[1] * jnp.exp(other[0] - highest)
    return jnp.concatenate([highest[None], summed[None], mine[2:] + other[2:]], axis=0)


def butterfly_merge(stats, axis, size, bit=1, other=None):
    own = lax.axis_index(axis)
    while bit < size:
        if other is None:
            other = lax.ppermute(stats, axis, [(i, i ^ bit) for i in range(size)])
        lower = (own & bit) == 0
        stats = merge_pair(jnp.where(lower, stats, other), jnp.where(lower, other, stats))
        other = None
        bit *= 2
    return stats


def butterfly_sum(values, axis, size):
    own = lax.axis_index(axis)
    bit = 1
    while bit < size:
        other = lax.ppermute(values, axis, [(i, i ^ bit) for i in range(size)])
        lower = (own & bit) == 0
        values = jnp.where(lower, values, other) + jnp.where(lower, other, values)
        bit *= 2
    return values


def ring_position(offset, size):
    return (offset + size // 2) % size


def ring_gather(shard, axis, size):
    forward = [(i, (i + 1) % size) for i in range(size)]
    backward = [(i, (i - 1) % size) for i in range(size)]
    parts = [None] * size
    parts[ring_position(0, size)] = shard
    ahead = shard
    behind = shard
    forward_steps = size // 2
    backward_steps = size - 1 - forward_steps
    for step in range(1, forward_steps + 1):
        ahead = lax.ppermute(ahead, axis, forward)
        parts[ring_position(-step, size)] = ahead
        if step <= backward_steps:
            behind = lax.ppermute(behind, axis, backward)
            parts[ring_position(step, size)] = behind
    return parts


def two_stage_reduce_scatter(grad_cols, extra, axis, size, shard_rows):
    pair_count, _, width = grad_cols.shape
    own = lax.axis_index(axis)
    parity = own % 2
    chips = size // 2
    by_chip = grad_cols.reshape(pair_count, chips, 2, shard_rows, width)
    keep = lax.dynamic_index_in_dim(by_chip, parity, axis=2, keepdims=False)
    send = lax.dynamic_index_in_dim(by_chip, 1 - parity, axis=2, keepdims=False)
    body_rows = pair_count * chips * shard_rows
    send = jnp.concatenate([send.reshape(body_rows, width), extra], axis=0)
    got = lax.ppermute(send, axis, [(i, i ^ 1) for i in range(size)])
    summed = keep + got[:body_rows].reshape(pair_count, chips, shard_rows, width)
    carried = extra + got[body_rows:]
    chip = own // 2
    ring = [(i, (i + 2) % size) for i in range(size)]
    chunk_rows = pair_count * shard_rows

    def addend(target):
        block = lax.dynamic_index_in_dim(summed, target % chips, axis=1, keepdims=False)
        return jnp.concatenate([block.reshape(chunk_rows, width), carried], axis=0)

    running = addend(chip - 1)
    for step in range(1, chips):
        running = lax.ppermute(running, axis, ring) + addend(chip - 1 - step)
    return running[:chunk_rows].reshape(pair_count, shard_rows, width), running[chunk_rows]


def per_device(anchor, partner, counts, pair_scale):
    pair_count, shard_rows, model_width = anchor.shape
    score_scale = 4.0 / math.sqrt(model_width)
    dp_size = lax.axis_size("dp")
    pair_size = lax.axis_size("pair")
    dp_index = lax.axis_index("dp")
    pair_place = lax.axis_index("pair")
    own_first = (dp_index * pair_size + pair_place) * shard_rows
    offsets = jnp.arange(shard_rows, dtype=jnp.int32)
    own_valid = own_first + offsets[None, :] < counts[:, None]
    positive = (
        jnp.sum(anchor.astype(jnp.float32) * partner.astype(jnp.float32), axis=2) * score_scale
    )
    own_positive = jnp.sum(jnp.where(own_valid, positive, 0.0), axis=1)

    row_set = lax.all_gather(anchor, "pair", axis=1, tiled=True)
    col_set = jnp.concatenate(ring_gather(partner, "dp", dp_size), axis=1)
    col_set = jnp.roll(col_set, (dp_index - dp_size // 2) * shard_rows, axis=1)
    row_count = row_set.shape[1]
    col_count = col_set.shape[1]
    row_global = dp_index * row_count + jnp.arange(row_count, dtype=jnp.int32)
    col_first = (jnp.arange(dp_size, dtype=jnp.int32) * pair_size + pair_place) * shard_rows
    col_global = (col_first[:, None] + offsets[None, :]).reshape(-1)
    row_valid = row_global[None, :] < counts[:, None]
    col_valid = col_global[None, :] < counts[:, None]
    inside = row_valid[:, :, None] & col_valid[:, None, :]

    scores = (
        jnp.einsum("prd,pcd->prc", row_set, col_set, preferred_element_type=jnp.float32)
        * score_scale
    )
    masked = jnp.where(inside, scores, NEG)
    row_high = jnp.max(masked, axis=2)
    row_sum = jnp.sum(jnp.where(inside, jnp.exp(masked - row_high[:, :, None]), 0.0), axis=2)
    col_high = jnp.max(masked, axis=1)
    col_sum = jnp.sum(jnp.where(inside, jnp.exp(masked - col_high[:, None, :]), 0.0), axis=1)

    lanes = jnp.arange(row_count, dtype=jnp.int32)[None, :]
    carried = jnp.where(lanes == 0, own_positive[:, None], 0.0)
    row_stats = jnp.stack([row_high, row_sum, carried])
    row_first = lax.ppermute(row_stats, "pair", [(i, i ^ 1) for i in range(pair_size)])
    col_stats, row_first = lax.optimization_barrier((jnp.stack([col_high, col_sum]), row_first))
    row_stats = butterfly_merge(row_stats, "pair", pair_size, 1, row_first)
    row_high, row_sum, carried = row_stats[0], row_stats[1], row_stats[2]
    row_lse = jnp.where(row_valid, row_high + jnp.log(jnp.where(row_valid, row_sum, 1.0)), 0.0)
    row_part = jnp.sum(row_lse, axis=1) - 2.0 * carried[:, 0]

    col_stats = butterfly_merge(col_stats, "dp", dp_size)
    col_high, col_sum = col_stats[0], col_stats[1]
    col_lse = jnp.where(col_valid, col_high + jnp.log(jnp.where(col_valid, col_sum, 1.0)), 0.0)

    prob_row = jnp.where(inside, jnp.exp(scores - row_lse[:, :, None]), 0.0)
    prob_col = jnp.where(inside, jnp.exp(scores - col_lse[:, None, :]), 0.0)
    weights = (pair_scale[:, None, None] * 0.5 * (prob_row + prob_col)).astype(jnp.bfloat16)
    weights = lax.optimization_barrier(weights)
    grad_rows = (
        jnp.einsum("prc,pcd->prd", weights, col_set, preferred_element_type=jnp.float32)
        * score_scale
    )
    grad_cols = (
        jnp.einsum("prc,prd->pcd", weights, row_set, preferred_element_type=jnp.float32)
        * score_scale
    )
    anchor_part = lax.psum_scatter(grad_rows, "pair", scatter_dimension=1, tiled=True)

    width_lanes = jnp.arange(model_width, dtype=jnp.int32)[None, :]
    slots = (jnp.arange(pair_count, dtype=jnp.int32) * dp_size + dp_index)[:, None]
    loss_row = jnp.sum(jnp.where(width_lanes == slots, row_part[:, None], 0.0), axis=0)
    extra = jnp.concatenate([loss_row[None], jnp.zeros((7, model_width), jnp.float32)], axis=0)
    partner_part, loss_row = two_stage_reduce_scatter(grad_cols, extra, "dp", dp_size, shard_rows)
    row_parts = loss_row[: pair_count * dp_size].reshape(pair_count, dp_size)

    col_total = butterfly_sum(jnp.sum(col_lse, axis=1), "pair", pair_size)
    totals = col_total + jnp.sum(row_parts, axis=1)
    loss_value = jnp.sum(totals / (2.0 * counts.astype(jnp.float32))) / pair_count

    own_term = (pair_scale * score_scale)[:, None, None]
    keep_rows = own_valid[:, :, None]
    anchor_out = jnp.where(keep_rows, anchor_part - own_term * partner.astype(jnp.float32), 0.0)
    partner_out = jnp.where(keep_rows, partner_part - own_term * anchor.astype(jnp.float32), 0.0)
    return (loss_value, anchor_out, partner_out)


def solution(mesh):
    in_specs = (P(None, ("dp", "pair"), None), P(None, ("dp", "pair"), None), P(), P())
    out_specs = (P(), P(None, ("dp", "pair"), None), P(None, ("dp", "pair"), None))
    return jax.shard_map(
        per_device, mesh=mesh, in_specs=in_specs, out_specs=out_specs, check_vma=False
    )
```

```python
import math

import jax
import jax.numpy as jnp
from jax import lax
from jax.sharding import PartitionSpec as P

NEG = -1e30


def merge_pair(mine, other):
    highest = jnp.maximum(mine[0], other[0])
    summed = mine[1] * jnp.exp(mine[0] - highest) + other[1] * jnp.exp(other[0] - highest)
    return jnp.concatenate([highest[None], summed[None], mine[2:] + other[2:]], axis=0)


def butterfly_merge(stats, axis, size):
    own = lax.axis_index(axis)
    bit = 1
    while bit < size:
        other = lax.ppermute(stats, axis, [(i, i ^ bit) for i in range(size)])
        lower = (own & bit) == 0
        stats = merge_pair(jnp.where(lower, stats, other), jnp.where(lower, other, stats))
        bit *= 2
    return stats


def butterfly_sum(values, axis, size):
    own = lax.axis_index(axis)
    bit = 1
    while bit < size:
        other = lax.ppermute(values, axis, [(i, i ^ bit) for i in range(size)])
        lower = (own & bit) == 0
        values = jnp.where(lower, values, other) + jnp.where(lower, other, values)
        bit *= 2
    return values


def ring_position(offset, size):
    return (offset + size // 2) % size


def ring_gather(shard, axis, size):
    forward = [(i, (i + 1) % size) for i in range(size)]
    backward = [(i, (i - 1) % size) for i in range(size)]
    parts = [None] * size
    parts[ring_position(0, size)] = shard
    ahead = shard
    behind = shard
    forward_steps = size // 2
    backward_steps = size - 1 - forward_steps
    for step in range(1, forward_steps + 1):
        ahead = lax.ppermute(ahead, axis, forward)
        parts[ring_position(-step, size)] = ahead
        if step <= backward_steps:
            behind = lax.ppermute(behind, axis, backward)
            parts[ring_position(step, size)] = behind
    return parts


def two_stage_reduce_scatter(grad_cols, extra, axis, size, shard_rows):
    pair_count, _, width = grad_cols.shape
    own = lax.axis_index(axis)
    parity = own % 2
    chips = size // 2
    by_chip = grad_cols.reshape(pair_count, chips, 2, shard_rows, width)
    keep = lax.dynamic_index_in_dim(by_chip, parity, axis=2, keepdims=False)
    send = lax.dynamic_index_in_dim(by_chip, 1 - parity, axis=2, keepdims=False)
    body_rows = pair_count * chips * shard_rows
    send = jnp.concatenate([send.reshape(body_rows, width), extra], axis=0)
    got = lax.ppermute(send, axis, [(i, i ^ 1) for i in range(size)])
    summed = keep + got[:body_rows].reshape(pair_count, chips, shard_rows, width)
    carried = extra + got[body_rows:]
    chip = own // 2
    sign = 1 - 2 * parity
    ring = [(i, (i + (2 if i % 2 == 0 else -2)) % size) for i in range(size)]
    chunk_rows = pair_count * shard_rows

    def addend(target):
        block = lax.dynamic_index_in_dim(summed, target % chips, axis=1, keepdims=False)
        return jnp.concatenate([block.reshape(chunk_rows, width), carried], axis=0)

    running = addend(chip - sign)
    for step in range(1, chips):
        running = lax.ppermute(running, axis, ring) + addend(chip - sign * (1 + step))
    return running[:chunk_rows].reshape(pair_count, shard_rows, width), running[chunk_rows]


def pair_ring_reduce_scatter(blocks, side):
    pair_count, _, rows, width = blocks.shape
    dp_size = lax.axis_size("dp")
    pair_size = side * side
    parity = lax.axis_index("dp") % 2
    sign = 1 - 2 * parity
    place = lax.axis_index("pair")
    z_own = place // side
    y_own = place % side

    def ring(step_of):
        return [(d * pair_size + k, d * pair_size + step_of(k, 1 if d % 2 == 0 else -1))
                for d in range(dp_size) for k in range(pair_size)]

    along_y = ring(lambda k, s: (k // side) * side + (k % side + s) % side)
    along_z = ring(lambda k, s: ((k // side + s) % side) * side + k % side)
    grid = blocks.reshape(pair_count, side, side, rows, width)

    def y_part(step):
        return lax.dynamic_index_in_dim(grid, (y_own - sign * (1 + step)) % side, 2, False)

    running = y_part(0)
    for step in range(1, side):
        running = lax.ppermute(running, ("dp", "pair"), along_y) + y_part(step)

    def z_part(step):
        return lax.dynamic_index_in_dim(running, (z_own - sign * (1 + step)) % side, 1, False)

    total = z_part(0)
    for step in range(1, side):
        total = lax.ppermute(total, ("dp", "pair"), along_z) + z_part(step)
    return total


def per_device(anchor, partner, counts, pair_scale):
    pair_count, shard_rows, model_width = anchor.shape
    score_scale = 4.0 / math.sqrt(model_width)
    dp_size = lax.axis_size("dp")
    pair_size = lax.axis_size("pair")
    dp_index = lax.axis_index("dp")
    pair_place = lax.axis_index("pair")
    own_first = (dp_index * pair_size + pair_place) * shard_rows
    offsets = jnp.arange(shard_rows, dtype=jnp.int32)
    own_valid = own_first + offsets[None, :] < counts[:, None]
    positive = (
        jnp.sum(anchor.astype(jnp.float32) * partner.astype(jnp.float32), axis=2) * score_scale
    )
    own_positive = jnp.sum(jnp.where(own_valid, positive, 0.0), axis=1)

    row_set = lax.all_gather(anchor, "pair", axis=1, tiled=True)
    col_set = jnp.concatenate(ring_gather(partner, "dp", dp_size), axis=1)
    col_set = jnp.roll(col_set, (dp_index - dp_size // 2) * shard_rows, axis=1)
    row_count = row_set.shape[1]
    col_count = col_set.shape[1]
    row_global = dp_index * row_count + jnp.arange(row_count, dtype=jnp.int32)
    col_first = (jnp.arange(dp_size, dtype=jnp.int32) * pair_size + pair_place) * shard_rows
    col_global = (col_first[:, None] + offsets[None, :]).reshape(-1)
    row_valid = row_global[None, :] < counts[:, None]
    col_valid = col_global[None, :] < counts[:, None]
    inside = row_valid[:, :, None] & col_valid[:, None, :]

    scores = (
        jnp.einsum("prd,pcd->prc", row_set, col_set, preferred_element_type=jnp.float32)
        * score_scale
    )
    masked = jnp.where(inside, scores, NEG)
    row_high = jnp.max(masked, axis=2)
    row_sum = jnp.sum(jnp.where(inside, jnp.exp(masked - row_high[:, :, None]), 0.0), axis=2)
    col_high = jnp.max(masked, axis=1)
    col_sum = jnp.sum(jnp.where(inside, jnp.exp(masked - col_high[:, None, :]), 0.0), axis=1)

    col_stats = butterfly_merge(jnp.stack([col_high, col_sum]), "dp", dp_size)
    col_high, col_sum = col_stats[0], col_stats[1]
    col_lse = jnp.where(col_valid, col_high + jnp.log(jnp.where(col_valid, col_sum, 1.0)), 0.0)

    lanes = jnp.arange(row_count, dtype=jnp.int32)[None, :]
    carried = jnp.where(lanes == 0, own_positive[:, None], 0.0)
    row_stats = butterfly_merge(jnp.stack([row_high, row_sum, carried]), "pair", pair_size)
    row_high, row_sum, carried = row_stats[0], row_stats[1], row_stats[2]
    row_lse = jnp.where(row_valid, row_high + jnp.log(jnp.where(row_valid, row_sum, 1.0)), 0.0)
    row_part = jnp.sum(row_lse, axis=1) - 2.0 * carried[:, 0]

    prob_row = jnp.where(inside, jnp.exp(scores - row_lse[:, :, None]), 0.0)
    prob_col = jnp.where(inside, jnp.exp(scores - col_lse[:, None, :]), 0.0)
    weights = (pair_scale[:, None, None] * 0.5 * (prob_row + prob_col)).astype(jnp.bfloat16)
    weights = lax.optimization_barrier(weights)
    ring_width = model_width // 8
    main_width = model_width - ring_width
    col_main = col_set[:, :, :main_width]
    col_ring = col_set[:, :, main_width:]
    grad_rows = (
        jnp.einsum("prc,pcd->prd", weights, col_main, preferred_element_type=jnp.float32)
        * score_scale
    )
    grad_ring = (
        jnp.einsum("prc,pcd->prd", weights, col_ring, preferred_element_type=jnp.float32)
        * score_scale
    )
    grad_cols = (
        jnp.einsum("prc,prd->pcd", weights, row_set, preferred_element_type=jnp.float32)
        * score_scale
    )
    anchor_part = lax.psum_scatter(grad_rows, "pair", scatter_dimension=1, tiled=True)
    side = math.isqrt(pair_size)
    ring_part = pair_ring_reduce_scatter(
        grad_ring.reshape(pair_count, pair_size, shard_rows, ring_width), side
    )
    anchor_part = jnp.concatenate([anchor_part, ring_part], axis=2)

    width_lanes = jnp.arange(model_width, dtype=jnp.int32)[None, :]
    slots = (jnp.arange(pair_count, dtype=jnp.int32) * dp_size + dp_index)[:, None]
    loss_row = jnp.sum(jnp.where(width_lanes == slots, row_part[:, None], 0.0), axis=0)
    extra = jnp.concatenate([loss_row[None], jnp.zeros((7, model_width), jnp.float32)], axis=0)
    partner_part, loss_row = two_stage_reduce_scatter(grad_cols, extra, "dp", dp_size, shard_rows)
    row_parts = loss_row[: pair_count * dp_size].reshape(pair_count, dp_size)

    col_total = butterfly_sum(jnp.sum(col_lse, axis=1), "pair", pair_size)
    totals = col_total + jnp.sum(row_parts, axis=1)
    loss_value = jnp.sum(totals / (2.0 * counts.astype(jnp.float32))) / pair_count

    own_term = (pair_scale * score_scale)[:, None, None]
    keep_rows = own_valid[:, :, None]
    anchor_out = jnp.where(keep_rows, anchor_part - own_term * partner.astype(jnp.float32), 0.0)
    partner_out = jnp.where(keep_rows, partner_part - own_term * anchor.astype(jnp.float32), 0.0)
    return (loss_value, anchor_out, partner_out)


def solution(mesh):
    in_specs = (P(None, ("dp", "pair"), None), P(None, ("dp", "pair"), None), P(), P())
    out_specs = (P(), P(None, ("dp", "pair"), None), P(None, ("dp", "pair"), None))
    return jax.shard_map(
        per_device, mesh=mesh, in_specs=in_specs, out_specs=out_specs, check_vma=False
    )
```
